256 devices in a mesh: bus: 16 (over y, z_hi), line: 16 (over z_lo, x, core).
Axes of the slice: x: 4, y: 4, z: 8 (z_hi: 4, z_lo: 2; z = z_hi * 2 + z_lo), core: 2. Of those that a mesh axis runs over, the one named last changes fastest.
Arguments:
- generation: bfloat16 [1024, 16384], P(None, 'bus'), may hold values from -6 to 6
- profiles: float32 [24, 16384], P(None, 'bus'), may hold values from -5 to 5
- scen_profile: int32 [1024], replicated, may hold values from 0 to 23
- ptdf: bfloat16 [16384, 16384], P('line', 'bus'), may hold values from -0.046875 to 0.046875
- lodf: float32 [6144, 512], P('line'), may hold values from -1 to 1
- limits: float32 [6144], P('line'), may hold values from 0.5 to 2
- monitored: int32 [6144], P('line'), may hold values from 0 to 16383, as said below
- outages: int32 [512], replicated, may hold values from 0 to 16383, as said below
- cost_quad: float32 [16384], P('bus'), may hold values from 0.5 to 2
Outputs:
- gradient: bfloat16 [1024, 16384], P('line', 'bus')
- outage_flow: float32 [1024, 512], P('bus')
- outage_sens: float32 [1024, 512], P('bus')
The draws below stay inside these ranges and needn't reach their ends.
Inputs may be any that keep to these rules, and one draw needn't show every extreme that they name: `monitored`: the entries with positions k * 384 to (k + 1) * 384 - 1 are distinct line ids of the k-th block of 1024 lines (ids k * 1024 to (k + 1) * 1024 - 1). `outages`: distinct line ids; how many fall in each block of 1024 lines varies from block to block.
All inputs are finite; a program needn't handle non-finite values.
Results may differ from the reference program's by a relative error of at most 0.0029.
Values may be sent and summed in bfloat16 or wider, within the bound.
No kernel may reach another device: no remote copies, remote signals or barrier semaphores. Data moves between devices by JAX's collectives and lax.ppermute only.
A program may use at most 64 MiB of HBM per device.

```python
import math
import jax
import jax.numpy as jnp
from jax import lax

LINES = 16384
BUSES = 16384
OUTAGES = 512
PROFILES = 24
MON_DEV = 384
SCEN = 1024
MONITORED = 6144
N_BUS = 16
N_LINE = 16


def draw_monitored(key, part):
    line_rows = LINES // N_LINE

    def one_block(group):
        order = jax.random.permutation(jax.random.fold_in(key, group), line_rows)
        return order[:MON_DEV].astype(jnp.int32) + group * line_rows
    return jax.vmap(one_block)(jnp.arange(N_LINE, dtype=jnp.int32)).reshape(-1)


def draw_outages(key, part):
    line_rows = LINES // N_LINE
    tilted = jax.random.randint(jax.random.fold_in(key, 11), (N_LINE,), 0, 4)
    ranking = jax.random.permutation(jax.random.fold_in(key, 12), LINES).astype(jnp.int32)
    line_ids = jnp.arange(LINES, dtype=jnp.int32)
    scores = (ranking + tilted[line_ids // line_rows] * (LINES // 64)) * LINES + line_ids
    chosen = lax.top_k(scores, OUTAGES)[1]
    return chosen.astype(jnp.int32)


def with_ends(values, rng, least, largest):
    extent = values.shape
    spot = [jax.random.randint(jax.random.fold_in(rng, axis), (), 0, extent[axis]) for axis in range(len(extent))]
    values = values.at[tuple(spot)].set(least)
    longest = extent.index(max(extent))
    spot[longest] = (spot[longest] + 1) % extent[longest]
    return values.at[tuple(spot)].set(largest)


def block_levels(own_key, shape, split, least, largest):
    def one(position, blocks):
        heights = jax.random.uniform(jax.random.fold_in(jax.random.fold_in(own_key, 6), position), (blocks,), jnp.float32, least / len(split), largest / len(split))
        return jnp.repeat(jnp.exp(heights), shape[position] // blocks).reshape((-1,) + (1,) * (len(shape) - position - 1))

    loudness = one(*split[0])
    for cut in split[1:]:
        loudness = loudness * one(*cut)
    return loudness


def normal_values(rng, shape, spread, limit, cuts=(), held_as=jnp.bfloat16):
    loudness = block_levels(rng, shape, cuts, -0.22, 0.18) if cuts else 1.0
    result = jax.random.normal(rng, shape, jnp.float32) * spread * loudness
    return jnp.minimum(jnp.maximum(result, -limit), limit).astype(held_as)


def setup_inputs(seed: int = 0) -> dict:
    keys = jax.random.split(jax.random.key(seed), 10)
    generation = normal_values(keys[0], (SCEN, BUSES), 1.0, 6.0, ((1, 16),))
    profiles = normal_values(keys[1], (PROFILES, BUSES), 0.7, 5.0, ((1, 16),), jnp.float32)
    scen_profile = with_ends(jax.random.randint(keys[2], (SCEN,), 0, PROFILES), jax.random.fold_in(keys[2], 1), 0, PROFILES - 1).astype(jnp.int32)
    ptdf = normal_values(keys[3], (LINES, BUSES), BUSES ** -0.5, 0.046875, ((0, 16), (1, 16)))
    lodf = jnp.clip(jax.random.uniform(keys[4], (MONITORED, OUTAGES), jnp.float32, -1.0, 1.0) * block_levels(keys[4], (MONITORED, OUTAGES), ((0, 16),), -0.4, 0.0), -1.0, 1.0)
    limits = jnp.clip(jnp.exp(math.log(2.0) - 1.3862944 * jax.random.uniform(keys[5], (MONITORED,), jnp.float32) ** block_levels(keys[5], (MONITORED,), ((0, 16),), -0.2, 0.2)), 0.5, 2.0)
    monitored = draw_monitored(jax.random.fold_in(keys[9], 71), 0)
    outages = draw_outages(jax.random.fold_in(keys[9], 71), 0)
    cost_quad = jnp.clip(jnp.exp(math.log(2.0) - 1.3862944 * jax.random.uniform(keys[8], (BUSES,), jnp.float32) ** block_levels(keys[8], (BUSES,), ((0, 16),), -0.2, 0.2)), 0.5, 2.0)
    return dict(generation=generation, profiles=profiles, scen_profile=scen_profile, ptdf=ptdf, lodf=lodf, limits=limits, monitored=monitored, outages=outages, cost_quad=cost_quad)


sharpness = 4.0

def contingency(pieces, lodf, limits):
    base_block, outage_block = pieces
    post_flow = base_block[:, :, None] + lodf[None, :, :] * outage_block[:, None, :]
    bounds = limits[None, :, None]
    raw_slope = jax.nn.sigmoid(sharpness * (post_flow - bounds)) - jax.nn.sigmoid(sharpness * (-post_flow - bounds))
    direct = lax.optimization_barrier(jnp.sum(raw_slope, axis=2)) / OUTAGES
    sens_total = jnp.einsum('smk,mk->sk', raw_slope, lodf, precision=lax.Precision.HIGHEST)
    return (direct, sens_total)

def reference(generation, profiles, scen_profile, ptdf, lodf, limits, monitored, outages, cost_quad):
    injection = (generation.astype(jnp.float32) - profiles[scen_profile]).astype(jnp.bfloat16)
    bus_width = BUSES // N_BUS
    line_width = LINES // N_LINE

    def flow_group(group, running):
        columns = lax.dynamic_slice_in_dim(ptdf, group * bus_width, bus_width, 1).astype(jnp.float32)
        inputs = lax.dynamic_slice_in_dim(injection, group * bus_width, bus_width, 1).astype(jnp.float32)
        return running + jnp.dot(inputs, columns.T, precision=lax.Precision.HIGHEST)
    flows = lax.fori_loop(0, N_BUS, flow_group, jnp.zeros((SCEN, LINES), jnp.float32))
    base = flows[:, monitored]
    outflow = flows[:, outages]
    block_size = math.gcd(SCEN, 4)
    base_blocks = base.reshape(SCEN // block_size, block_size, MONITORED)
    outage_blocks = outflow.reshape(SCEN // block_size, block_size, OUTAGES)
    direct, sens_total = lax.map(lambda pieces: contingency(pieces, lodf, limits), (base_blocks, outage_blocks))
    direct = direct.reshape(SCEN, MONITORED)
    sens_total = sens_total.reshape(SCEN, OUTAGES)
    backward = sens_total / OUTAGES
    outage_sens = sens_total / math.sqrt(MONITORED)
    adjoint = jnp.zeros((SCEN, LINES), jnp.float32).at[:, monitored].add(direct)
    adjoint = adjoint.at[:, outages].add(backward).astype(jnp.bfloat16)

    def grad_group(group, running):
        row_block = lax.dynamic_slice_in_dim(ptdf, group * line_width, line_width, 0).astype(jnp.float32)
        inputs = lax.dynamic_slice_in_dim(adjoint, group * line_width, line_width, 1).astype(jnp.float32)
        return running + jnp.dot(inputs, row_block, precision=lax.Precision.HIGHEST)
    pushed = lax.fori_loop(0, N_LINE, grad_group, jnp.zeros((SCEN, BUSES), jnp.float32))
    gradient = (cost_quad[None, :] * generation.astype(jnp.float32) + pushed).astype(jnp.bfloat16)
    return (gradient, outflow, outage_sens)
```

```python
import math

import jax
import jax.numpy as jnp
from jax import lax
from jax.sharding import PartitionSpec as P

sharpness = 4.0


def contingency(pieces, lodf, limits, outage_total):
    base_block, outage_block = pieces
    post_flow = base_block[:, :, None] + lodf[None, :, :] * outage_block[:, None, :]
    bounds = limits[None, :, None]
    raw_slope = jax.nn.sigmoid(sharpness * (post_flow - bounds)) - jax.nn.sigmoid(
        sharpness * (-post_flow - bounds)
    )
    direct = jnp.sum(raw_slope, axis=2) / outage_total
    sens_part = jnp.einsum("smk,mk->sk", raw_slope, lodf, precision=lax.Precision.HIGHEST)
    return (direct, sens_part)


def on_device(
    generation, profiles, scen_profile, ptdf, lodf, limits, monitored, outages, cost_quad
):
    line_count = lax.axis_size("line")
    profile_count = profiles.shape[0]
    profile_pick = (
        scen_profile[:, None] == jnp.arange(profile_count, dtype=jnp.int32)[None, :]
    ).astype(jnp.float32)
    loads = jnp.dot(profile_pick, profiles, precision=lax.Precision.HIGHEST)
    injection = (generation.astype(jnp.float32) - loads).astype(jnp.bfloat16)
    scen_rows = injection.shape[0] // lax.axis_size("bus")
    line_rows = ptdf.shape[0]
    first_line = lax.axis_index("line") * line_rows
    local_monitored = monitored - first_line
    monitor_count = monitored.shape[0]
    outage_total = outages.shape[0]
    monitored_total = monitor_count * line_count

    rel_outages = outages - first_line
    in_block = (rel_outages >= 0) & (rel_outages < line_rows)
    outage_rows = jnp.where(
        in_block[:, None],
        jnp.take(ptdf, jnp.clip(rel_outages, 0, line_rows - 1), axis=0),
        jnp.zeros((), ptdf.dtype),
    )
    my_outage_rows = lax.psum_scatter(outage_rows, "line", scatter_dimension=0, tiled=True)
    monitored_rows = jnp.take(ptdf, local_monitored, axis=0)
    rows = jnp.concatenate([monitored_rows, my_outage_rows], axis=0)

    flow_part = lax.dot_general(
        injection, rows, (((1,), (1,)), ((), ())), preferred_element_type=jnp.float32
    )
    flow_field = lax.psum_scatter(flow_part, "bus", scatter_dimension=0, tiled=True)
    base = flow_field[:, :monitor_count]
    outflow = lax.all_gather(flow_field[:, monitor_count:], "line", axis=1, tiled=True)

    block_size = math.gcd(scen_rows, 4)
    base_blocks = base.reshape(scen_rows // block_size, block_size, monitor_count)
    outage_blocks = outflow.reshape(scen_rows // block_size, block_size, outage_total)
    direct, sens_part = lax.map(
        lambda pieces: contingency(pieces, lodf, limits, outage_total), (base_blocks, outage_blocks)
    )
    direct = direct.reshape(scen_rows, monitor_count)
    sens_part = sens_part.reshape(scen_rows, outage_total)

    matches = (outages[:, None] == monitored[None, :]).astype(jnp.float32)
    flag_part = jnp.sum(matches, axis=1)
    extended = jnp.concatenate(
        [sens_part, flag_part[None, :], jnp.zeros((7, outage_total), jnp.float32)], axis=0
    )
    mine = lax.psum_scatter(extended, "line", scatter_dimension=1, tiled=True)
    sens_mine = mine[:scen_rows]
    flag_mine = mine[scen_rows]
    sens_total = lax.all_gather(sens_mine, "line", axis=1, tiled=True)
    backward = sens_total / outage_total
    outage_sens = sens_total / math.sqrt(monitored_total)

    adjoint_monitored = (
        direct + jnp.dot(backward, matches, precision=lax.Precision.HIGHEST)
    ).astype(jnp.bfloat16)
    adjoint_outage = jnp.where(
        flag_mine[None, :] > 0.5, 0.0, sens_mine / outage_total
    ).astype(jnp.bfloat16)
    piece = jnp.concatenate([adjoint_monitored, adjoint_outage], axis=1)
    all_piece = lax.all_gather(piece, "bus", axis=0, tiled=True)
    grad_rows = all_piece.shape[0] // line_count
    pushed = lax.psum_scatter(
        jnp.dot(all_piece, rows, preferred_element_type=jnp.float32),
        "line",
        scatter_dimension=0,
        tiled=True,
    )
    own_generation = lax.dynamic_slice_in_dim(
        generation, lax.axis_index("line") * grad_rows, grad_rows, 0
    ).astype(jnp.float32)
    gradient = (cost_quad[None, :] * own_generation + pushed).astype(jnp.bfloat16)
    return (gradient, outflow, outage_sens)


def solution(mesh):
    placed = (
        P(None, "bus"),
        P(None, "bus"),
        P(),
        P("line", "bus"),
        P("line", None),
        P("line"),
        P("line"),
        P(),
        P("bus"),
    )
    return jax.shard_map(
        on_device,
        mesh=mesh,
        in_specs=placed,
        out_specs=(P("line", "bus"), P("bus", None), P("bus", None)),
        check_vma=False,
    )
```

```python
import math

import jax
import jax.numpy as jnp
from jax import lax
from jax.sharding import PartitionSpec as P

sharpness = 4.0


def contingency(pieces, lodf, limits, outage_total):
    base_block, outage_block = pieces
    post_flow = base_block[:, :, None] + lodf[None, :, :] * outage_block[:, None, :]
    bounds = limits[None, :, None]
    raw_slope = jax.nn.sigmoid(sharpness * (post_flow - bounds)) - jax.nn.sigmoid(
        sharpness * (-post_flow - bounds)
    )
    direct = jnp.sum(raw_slope, axis=2) / outage_total
    sens_part = jnp.einsum("smk,mk->sk", raw_slope, lodf, precision=lax.Precision.HIGHEST)
    return (direct, sens_part)


def exchange_sum(values, axis, count):
    blocks = values.reshape((count, values.shape[0] // count) + values.shape[1:])
    return jnp.sum(lax.all_to_all(blocks, axis, 0, 0, tiled=False), axis=0)


def on_device(
    generation, profiles, scen_profile, ptdf, lodf, limits, monitored, outages, cost_quad
):
    line_count = lax.axis_size("line")
    profile_count = profiles.shape[0]
    profile_pick = (
        scen_profile[:, None] == jnp.arange(profile_count, dtype=jnp.int32)[None, :]
    ).astype(jnp.float32)
    loads = jnp.dot(profile_pick, profiles, precision=lax.Precision.HIGHEST)
    injection = (generation.astype(jnp.float32) - loads).astype(jnp.bfloat16)
    scen_rows = injection.shape[0] // lax.axis_size("bus")
    line_rows = ptdf.shape[0]
    first_line = lax.axis_index("line") * line_rows
    local_monitored = monitored - first_line
    monitor_count = monitored.shape[0]
    outage_total = outages.shape[0]
    monitored_total = monitor_count * line_count

    rel_outages = outages - first_line
    in_block = (rel_outages >= 0) & (rel_outages < line_rows)
    outage_rows = jnp.where(
        in_block[:, None],
        jnp.take(ptdf, jnp.clip(rel_outages, 0, line_rows - 1), axis=0),
        jnp.zeros((), ptdf.dtype),
    )
    my_outage_rows = exchange_sum(outage_rows, "line", line_count)
    monitored_rows = jnp.take(ptdf, local_monitored, axis=0)
    rows = jnp.concatenate([monitored_rows, my_outage_rows], axis=0)

    flow_part = lax.dot_general(
        injection, rows, (((1,), (1,)), ((), ())), preferred_element_type=jnp.float32
    )
    flow_field = exchange_sum(flow_part, "bus", lax.axis_size("bus"))
    base = flow_field[:, :monitor_count]
    outflow = lax.all_gather(flow_field[:, monitor_count:], "line", axis=1, tiled=True)

    block_size = math.gcd(scen_rows, 4)
    base_blocks = base.reshape(scen_rows // block_size, block_size, monitor_count)
    outage_blocks = outflow.reshape(scen_rows // block_size, block_size, outage_total)
    direct, sens_part = lax.map(
        lambda pieces: contingency(pieces, lodf, limits, outage_total), (base_blocks, outage_blocks)
    )
    direct = direct.reshape(scen_rows, monitor_count)
    sens_part = sens_part.reshape(scen_rows, outage_total)

    matches = (outages[:, None] == monitored[None, :]).astype(jnp.float32)
    flag_part = jnp.sum(matches, axis=1)
    extended = jnp.concatenate(
        [sens_part, flag_part[None, :], jnp.zeros((7, outage_total), jnp.float32)], axis=0
    )
    summed = jnp.sum(lax.all_gather(extended, "line", axis=0, tiled=False), axis=0)
    sens_total = summed[:scen_rows]
    out_share = outage_total // line_count
    share_start = lax.axis_index("line") * out_share
    sens_mine = lax.dynamic_slice_in_dim(sens_total, share_start, out_share, 1)
    flag_mine = lax.dynamic_slice_in_dim(summed[scen_rows], share_start, out_share, 0)
    backward = sens_total / outage_total
    outage_sens = sens_total / math.sqrt(monitored_total)

    adjoint_monitored = (
        direct + jnp.dot(backward, matches, precision=lax.Precision.HIGHEST)
    ).astype(jnp.bfloat16)
    adjoint_outage = jnp.where(
        flag_mine[None, :] > 0.5, 0.0, sens_mine / outage_total
    ).astype(jnp.bfloat16)
    piece = jnp.concatenate([adjoint_monitored, adjoint_outage], axis=1)
    bus_count = lax.axis_size("bus")
    all_piece = lax.all_to_all(
        jnp.broadcast_to(piece[None], (bus_count,) + piece.shape), "bus", 0, 0, tiled=False
    ).reshape(bus_count * piece.shape[0], piece.shape[1])
    grad_rows = all_piece.shape[0] // line_count
    pushed = exchange_sum(
        jnp.dot(all_piece, rows, preferred_element_type=jnp.float32), "line", line_count
    )
    own_generation = lax.dynamic_slice_in_dim(
        generation, lax.axis_index("line") * grad_rows, grad_rows, 0
    ).astype(jnp.float32)
    gradient = (cost_quad[None, :] * own_generation + pushed).astype(jnp.bfloat16)
    return (gradient, outflow, outage_sens)


def solution(mesh):
    placed = (
        P(None, "bus"),
        P(None, "bus"),
        P(),
        P("line", "bus"),
        P("line", None),
        P("line"),
        P("line"),
        P(),
        P("bus"),
    )
    return jax.shard_map(
        on_device,
        mesh=mesh,
        in_specs=placed,
        out_specs=(P("line", "bus"), P("bus", None), P("bus", None)),
        check_vma=False,
    )
```

```python
import math

import jax
import jax.numpy as jnp
from jax import lax
from jax.experimental import pallas as pl
from jax.sharding import PartitionSpec as P

sharpness = 4.0


def penalty_slopes(base, outflow, lodf, limits):
    scen_rows, monitor_count = base.shape
    outage_total = outflow.shape[1]
    sb = 8
    ch = 16
    blocks = scen_rows // sb
    half = sharpness / 2
    base3 = (half * base).reshape(blocks, sb, monitor_count).transpose(0, 2, 1)
    lodf2 = half * lodf
    lim2 = (half * limits).reshape(monitor_count, 1)

    def kernel(base_ref, out_ref, lodf_ref, lim_ref, direct_ref, sens_ref):
        for i in range(sb):
            flow_row = out_ref[i:i + 1, :]

            def body(c, acc):
                r = pl.multiple_of(c * ch, ch)
                weight = lodf_ref[pl.ds(r, ch), :]
                bound = lim_ref[pl.ds(r, ch), :]
                post = base_ref[pl.ds(r, ch), i:i + 1] + weight * flow_row
                slope = jnp.tanh(post - bound) + jnp.tanh(post + bound)
                direct_ref[pl.ds(r, ch), i:i + 1] = jnp.sum(slope, axis=1, keepdims=True)
                return acc + weight * slope

            acc = lax.fori_loop(0, monitor_count // ch, body,
                                jnp.zeros((ch, outage_total), jnp.float32))
            sens_ref[i:i + 1, :] = jnp.sum(acc, axis=0, keepdims=True)

    direct3, sens = pl.pallas_call(
        kernel,
        grid=(blocks,),
        in_specs=[
            pl.BlockSpec((None, monitor_count, sb), lambda g: (g, 0, 0)),
            pl.BlockSpec((sb, outage_total), lambda g: (g, 0)),
            pl.BlockSpec((monitor_count, outage_total), lambda g: (0, 0)),
            pl.BlockSpec((monitor_count, 1), lambda g: (0, 0)),
        ],
        out_specs=[
            pl.BlockSpec((None, monitor_count, sb), lambda g: (g, 0, 0)),
            pl.BlockSpec((sb, outage_total), lambda g: (g, 0)),
        ],
        out_shape=[
            jax.ShapeDtypeStruct((blocks, monitor_count, sb), jnp.float32),
            jax.ShapeDtypeStruct((scen_rows, outage_total), jnp.float32),
        ],
    )(base3, outflow, lodf2, lim2)
    direct = direct3.transpose(0, 2, 1).reshape(scen_rows, monitor_count) / (2.0 * outage_total)
    return direct, sens / (2.0 * half)

def exchange_sum(values, axis, count):
    blocks = values.reshape((count, values.shape[0] // count) + values.shape[1:])
    return jnp.sum(lax.all_to_all(blocks, axis, 0, 0, tiled=False), axis=0)


def on_device(
    generation, profiles, scen_profile, ptdf, lodf, limits, monitored, outages, cost_quad
):
    line_count = lax.axis_size("line")
    profile_count = profiles.shape[0]
    profile_pick = (
        scen_profile[:, None] == jnp.arange(profile_count, dtype=jnp.int32)[None, :]
    ).astype(jnp.float32)
    loads = jnp.dot(profile_pick, profiles, precision=lax.Precision.HIGHEST)
    injection = (generation.astype(jnp.float32) - loads).astype(jnp.bfloat16)
    scen_rows = injection.shape[0] // lax.axis_size("bus")
    line_rows = ptdf.shape[0]
    first_line = lax.axis_index("line") * line_rows
    local_monitored = monitored - first_line
    monitor_count = monitored.shape[0]
    outage_total = outages.shape[0]
    monitored_total = monitor_count * line_count

    rel_outages = outages - first_line
    in_block = (rel_outages >= 0) & (rel_outages < line_rows)
    outage_rows = jnp.where(
        in_block[:, None],
        jnp.take(ptdf, jnp.clip(rel_outages, 0, line_rows - 1), axis=0),
        jnp.zeros((), ptdf.dtype),
    )
    my_outage_rows = exchange_sum(outage_rows, "line", line_count)
    monitored_rows = jnp.take(ptdf, local_monitored, axis=0)
    rows = jnp.concatenate([monitored_rows, my_outage_rows], axis=0)

    flow_part = lax.dot_general(
        injection, rows, (((1,), (1,)), ((), ())), preferred_element_type=jnp.float32
    )
    flow_field = exchange_sum(flow_part, "bus", lax.axis_size("bus"))
    base = flow_field[:, :monitor_count]
    outflow = lax.all_gather(flow_field[:, monitor_count:], "line", axis=1, tiled=True)

    direct, sens_part = penalty_slopes(base, outflow, lodf, limits)

    matches = (outages[:, None] == monitored[None, :]).astype(jnp.float32)
    flag_part = jnp.sum(matches, axis=1)
    extended = jnp.concatenate(
        [sens_part, flag_part[None, :], jnp.zeros((7, outage_total), jnp.float32)], axis=0
    )
    out_share = outage_total // line_count
    shares = extended.reshape(extended.shape[0], line_count, out_share).transpose(1, 0, 2)
    mine = jnp.sum(lax.all_to_all(shares, "line", 0, 0, tiled=False), axis=0)
    sens_mine = mine[:scen_rows]
    flag_mine = mine[scen_rows]
    sens_total = lax.all_gather(sens_mine, "line", axis=1, tiled=True)
    backward = sens_total / outage_total
    outage_sens = sens_total / math.sqrt(monitored_total)

    adjoint_monitored = (
        direct + jnp.dot(backward, matches, precision=lax.Precision.HIGHEST)
    ).astype(jnp.bfloat16)
    adjoint_outage = jnp.where(
        flag_mine[None, :] > 0.5, 0.0, sens_mine / outage_total
    ).astype(jnp.bfloat16)
    piece = jnp.concatenate([adjoint_monitored, adjoint_outage], axis=1)
    bus_count = lax.axis_size("bus")
    all_piece = lax.all_to_all(
        jnp.broadcast_to(piece[None], (bus_count,) + piece.shape), "bus", 0, 0, tiled=False
    ).reshape(bus_count * piece.shape[0], piece.shape[1])
    grad_rows = all_piece.shape[0] // line_count
    pushed = exchange_sum(
        jnp.dot(all_piece, rows, preferred_element_type=jnp.float32), "line", line_count
    )
    own_generation = lax.dynamic_slice_in_dim(
        generation, lax.axis_index("line") * grad_rows, grad_rows, 0
    ).astype(jnp.float32)
    gradient = (cost_quad[None, :] * own_generation + pushed).astype(jnp.bfloat16)
    return (gradient, outflow, outage_sens)


def solution(mesh):
    placed = (
        P(None, "bus"),
        P(None, "bus"),
        P(),
        P("line", "bus"),
        P("line", None),
        P("line"),
        P("line"),
        P(),
        P("bus"),
    )
    return jax.shard_map(
        on_device,
        mesh=mesh,
        in_specs=placed,
        out_specs=(P("line", "bus"), P("bus", None), P("bus", None)),
        check_vma=False,
    )
```

```python
import math

import jax
import jax.numpy as jnp
from jax import lax
from jax.experimental import pallas as pl
from jax.sharding import PartitionSpec as P

sharpness = 4.0


def penalty_slopes(base, outflow, lodf, limits):
    scen_rows, monitor_count = base.shape
    outage_total = outflow.shape[1]
    sb = 8
    ch = 16
    lanes = 128
    blocks = scen_rows // sb
    half = sharpness / 2
    base3 = (half * base).reshape(blocks, sb, monitor_count).transpose(0, 2, 1)
    lodf2 = half * lodf
    lim2 = (half * limits).reshape(monitor_count, 1)

    def kernel(base_ref, out_ref, lodf_ref, lim_ref, direct_ref, sens_ref):
        for i in range(sb):
            flow_row = out_ref[i:i + 1, :]

            def body(c, acc):
                r = pl.multiple_of(c * ch, ch)
                weight = lodf_ref[pl.ds(r, ch), :]
                bound = lim_ref[pl.ds(r, ch), :]
                post = base_ref[pl.ds(r, ch), i:i + 1] + weight * flow_row
                slope = jnp.tanh(post - bound) + jnp.tanh(post + bound)
                folded = slope[:, 0:lanes]
                for q in range(1, outage_total // lanes):
                    folded = folded + slope[:, q * lanes:(q + 1) * lanes]
                direct_ref[i, pl.ds(r, ch), :] = folded
                return acc + weight * slope

            acc = lax.fori_loop(0, monitor_count // ch, body,
                                jnp.zeros((ch, outage_total), jnp.float32),
                                unroll=monitor_count // ch)
            sens_ref[i:i + 1, :] = jnp.sum(acc, axis=0, keepdims=True)

    direct_lanes, sens = pl.pallas_call(
        kernel,
        grid=(blocks,),
        in_specs=[
            pl.BlockSpec((None, monitor_count, sb), lambda g: (g, 0, 0)),
            pl.BlockSpec((sb, outage_total), lambda g: (g, 0)),
            pl.BlockSpec((monitor_count, outage_total), lambda g: (0, 0)),
            pl.BlockSpec((monitor_count, 1), lambda g: (0, 0)),
        ],
        out_specs=[
            pl.BlockSpec((sb, monitor_count, lanes), lambda g: (g, 0, 0)),
            pl.BlockSpec((sb, outage_total), lambda g: (g, 0)),
        ],
        out_shape=[
            jax.ShapeDtypeStruct((scen_rows, monitor_count, lanes), jnp.float32),
            jax.ShapeDtypeStruct((scen_rows, outage_total), jnp.float32),
        ],
    )(base3, outflow, lodf2, lim2)
    direct = jnp.sum(direct_lanes, axis=2) / (2.0 * outage_total)
    return direct, sens / (2.0 * half)


def exchange_sum(values, axis, count):
    blocks = values.reshape((count, values.shape[0] // count) + values.shape[1:])
    return jnp.sum(lax.all_to_all(blocks, axis, 0, 0, tiled=False), axis=0)


def on_device(
    generation, profiles, scen_profile, ptdf, lodf, limits, monitored, outages, cost_quad
):
    line_count = lax.axis_size("line")
    profile_count = profiles.shape[0]
    profile_pick = (
        scen_profile[:, None] == jnp.arange(profile_count, dtype=jnp.int32)[None, :]
    ).astype(jnp.float32)
    loads = jnp.dot(profile_pick, profiles, precision=lax.Precision.HIGHEST)
    injection = (generation.astype(jnp.float32) - loads).astype(jnp.bfloat16)
    scen_rows = injection.shape[0] // lax.axis_size("bus")
    line_rows = ptdf.shape[0]
    first_line = lax.axis_index("line") * line_rows
    local_monitored = monitored - first_line
    monitor_count = monitored.shape[0]
    outage_total = outages.shape[0]
    monitored_total = monitor_count * line_count

    rel_outages = outages - first_line
    in_block = (rel_outages >= 0) & (rel_outages < line_rows)
    outage_rows = jnp.where(
        in_block[:, None],
        jnp.take(ptdf, jnp.clip(rel_outages, 0, line_rows - 1), axis=0),
        jnp.zeros((), ptdf.dtype),
    )
    my_outage_rows = exchange_sum(outage_rows, "line", line_count)
    monitored_rows = jnp.take(ptdf, local_monitored, axis=0)
    rows = jnp.concatenate([monitored_rows, my_outage_rows], axis=0)

    flow_part = lax.dot_general(
        injection, rows, (((1,), (1,)), ((), ())), preferred_element_type=jnp.float32
    )
    flow_field = exchange_sum(flow_part, "bus", lax.axis_size("bus"))
    base = flow_field[:, :monitor_count]
    outflow = lax.all_gather(flow_field[:, monitor_count:], "line", axis=1, tiled=True)

    direct, sens_part = penalty_slopes(base, outflow, lodf, limits)

    matches = (outages[:, None] == monitored[None, :]).astype(jnp.float32)
    flag_part = jnp.sum(matches, axis=1)
    extended = jnp.concatenate(
        [sens_part, flag_part[None, :], jnp.zeros((7, outage_total), jnp.float32)], axis=0
    )
    out_share = outage_total // line_count
    shares = extended.reshape(extended.shape[0], line_count, out_share).transpose(1, 0, 2)
    mine = jnp.sum(lax.all_to_all(shares, "line", 0, 0, tiled=False), axis=0)
    sens_mine = mine[:scen_rows]
    flag_mine = mine[scen_rows]
    sens_total = lax.all_gather(sens_mine, "line", axis=1, tiled=True)
    backward = sens_total / outage_total
    outage_sens = sens_total / math.sqrt(monitored_total)

    adjoint_monitored = (
        direct + jnp.dot(backward, matches, precision=lax.Precision.HIGHEST)
    ).astype(jnp.bfloat16)
    adjoint_outage = jnp.where(
        flag_mine[None, :] > 0.5, 0.0, sens_mine / outage_total
    ).astype(jnp.bfloat16)
    piece = jnp.concatenate([adjoint_monitored, adjoint_outage], axis=1)
    bus_count = lax.axis_size("bus")
    all_piece = lax.all_to_all(
        jnp.broadcast_to(piece[None], (bus_count,) + piece.shape), "bus", 0, 0, tiled=False
    ).reshape(bus_count * piece.shape[0], piece.shape[1])
    grad_rows = all_piece.shape[0] // line_count
    pushed = exchange_sum(
        jnp.dot(all_piece, rows, preferred_element_type=jnp.float32), "line", line_count
    )
    own_generation = lax.dynamic_slice_in_dim(
        generation, lax.axis_index("line") * grad_rows, grad_rows, 0
    ).astype(jnp.float32)
    gradient = (cost_quad[None, :] * own_generation + pushed).astype(jnp.bfloat16)
    return (gradient, outflow, outage_sens)


def solution(mesh):
    placed = (
        P(None, "bus"),
        P(None, "bus"),
        P(),
        P("line", "bus"),
        P("line", None),
        P("line"),
        P("line"),
        P(),
        P("bus"),
    )
    return jax.shard_map(
        on_device,
        mesh=mesh,
        in_specs=placed,
        out_specs=(P("line", "bus"), P("bus", None), P("bus", None)),
        check_vma=False,
    )
```

```python
import math

import jax
import jax.numpy as jnp
from jax import lax
from jax.experimental import pallas as pl
from jax.sharding import PartitionSpec as P

sharpness = 4.0


def penalty_slopes(base, outflow, lodf, limits):
    scen_rows, monitor_count = base.shape
    outage_total = outflow.shape[1]
    sb = 8
    ch = 16
    lanes = 128
    blocks = scen_rows // sb
    half = sharpness / 2
    base3 = (half * base).reshape(blocks, sb, monitor_count).transpose(0, 2, 1)
    lodf2 = half * lodf
    lim2 = (half * limits).reshape(monitor_count, 1)

    def kernel(base_ref, out_ref, lodf_ref, lim_ref, direct_ref, sens_ref):
        for i in range(sb):
            flow_row = out_ref[i:i + 1, :]

            def body(c, acc):
                r = pl.multiple_of(c * ch, ch)
                weight = lodf_ref[pl.ds(r, ch), :]
                bound = lim_ref[pl.ds(r, ch), :]
                post = base_ref[pl.ds(r, ch), i:i + 1] + weight * flow_row
                slope = jnp.tanh(post - bound) + jnp.tanh(post + bound)
                folded = slope[:, 0:lanes]
                for q in range(1, outage_total // lanes):
                    folded = folded + slope[:, q * lanes:(q + 1) * lanes]
                direct_ref[i, pl.ds(r, ch), :] = folded
                return acc + weight * slope

            acc = lax.fori_loop(0, monitor_count // ch, body,
                                jnp.zeros((ch, outage_total), jnp.float32),
                                unroll=monitor_count // ch)
            sens_ref[i:i + 1, :] = jnp.sum(acc, axis=0, keepdims=True)

    direct_lanes, sens = pl.pallas_call(
        kernel,
        grid=(blocks,),
        in_specs=[
            pl.BlockSpec((None, monitor_count, sb), lambda g: (g, 0, 0)),
            pl.BlockSpec((sb, outage_total), lambda g: (g, 0)),
            pl.BlockSpec((monitor_count, outage_total), lambda g: (0, 0)),
            pl.BlockSpec((monitor_count, 1), lambda g: (0, 0)),
        ],
        out_specs=[
            pl.BlockSpec((sb, monitor_count, lanes), lambda g: (g, 0, 0)),
            pl.BlockSpec((sb, outage_total), lambda g: (g, 0)),
        ],
        out_shape=[
            jax.ShapeDtypeStruct((scen_rows, monitor_count, lanes), jnp.float32),
            jax.ShapeDtypeStruct((scen_rows, outage_total), jnp.float32),
        ],
    )(base3, outflow, lodf2, lim2)
    direct = jnp.sum(direct_lanes, axis=2) / (2.0 * outage_total)
    return direct, sens / (2.0 * half)


def exchange_sum(values, axis, count):
    blocks = values.reshape((count, values.shape[0] // count) + values.shape[1:])
    return jnp.sum(lax.all_to_all(blocks, axis, 0, 0, tiled=False), axis=0)


def gather_columns(values, axis, count):
    copies = jnp.broadcast_to(values[None], (count,) + values.shape)
    gathered = lax.all_to_all(copies, axis, 0, 0, tiled=False)
    return gathered.transpose(1, 0, 2).reshape(values.shape[0], count * values.shape[1])


def on_device(
    generation, profiles, scen_profile, ptdf, lodf, limits, monitored, outages, cost_quad
):
    line_count = lax.axis_size("line")
    profile_count = profiles.shape[0]
    profile_pick = (
        scen_profile[:, None] == jnp.arange(profile_count, dtype=jnp.int32)[None, :]
    ).astype(jnp.float32)
    loads = jnp.dot(profile_pick, profiles, precision=lax.Precision.HIGHEST)
    injection = (generation.astype(jnp.float32) - loads).astype(jnp.bfloat16)
    scen_rows = injection.shape[0] // lax.axis_size("bus")
    line_rows = ptdf.shape[0]
    first_line = lax.axis_index("line") * line_rows
    local_monitored = monitored - first_line
    monitor_count = monitored.shape[0]
    outage_total = outages.shape[0]
    monitored_total = monitor_count * line_count

    rel_outages = outages - first_line
    in_block = (rel_outages >= 0) & (rel_outages < line_rows)
    outage_rows = jnp.where(
        in_block[:, None],
        jnp.take(ptdf, jnp.clip(rel_outages, 0, line_rows - 1), axis=0),
        jnp.zeros((), ptdf.dtype),
    )
    my_outage_rows = exchange_sum(outage_rows, "line", line_count)
    monitored_rows = jnp.take(ptdf, local_monitored, axis=0)
    rows = jnp.concatenate([monitored_rows, my_outage_rows], axis=0)

    flow_part = lax.dot_general(
        injection, rows, (((1,), (1,)), ((), ())), preferred_element_type=jnp.float32
    )
    flow_field = exchange_sum(flow_part, "bus", lax.axis_size("bus"))
    base = flow_field[:, :monitor_count]
    outflow = gather_columns(flow_field[:, monitor_count:], "line", line_count)

    direct, sens_part = penalty_slopes(base, outflow, lodf, limits)

    matches = (outages[:, None] == monitored[None, :]).astype(jnp.float32)
    flag_part = jnp.sum(matches, axis=1)
    extended = jnp.concatenate(
        [sens_part, flag_part[None, :], jnp.zeros((7, outage_total), jnp.float32)], axis=0
    )
    out_share = outage_total // line_count
    shares = extended.reshape(extended.shape[0], line_count, out_share).transpose(1, 0, 2)
    mine = jnp.sum(lax.all_to_all(shares, "line", 0, 0, tiled=False), axis=0)
    sens_mine = mine[:scen_rows]
    flag_mine = mine[scen_rows]
    sens_total = gather_columns(sens_mine, "line", line_count)
    backward = sens_total / outage_total
    outage_sens = sens_total / math.sqrt(monitored_total)

    adjoint_monitored = (
        direct + jnp.dot(backward, matches, precision=lax.Precision.HIGHEST)
    ).astype(jnp.bfloat16)
    adjoint_outage = jnp.where(
        flag_mine[None, :] > 0.5, 0.0, sens_mine / outage_total
    ).astype(jnp.bfloat16)
    piece = jnp.concatenate([adjoint_monitored, adjoint_outage], axis=1)
    bus_count = lax.axis_size("bus")
    all_piece = lax.all_to_all(
        jnp.broadcast_to(piece[None], (bus_count,) + piece.shape), "bus", 0, 0, tiled=False
    ).reshape(bus_count * piece.shape[0], piece.shape[1])
    grad_rows = all_piece.shape[0] // line_count
    pushed = exchange_sum(
        jnp.dot(all_piece, rows, preferred_element_type=jnp.float32), "line", line_count
    )
    own_generation = lax.dynamic_slice_in_dim(
        generation, lax.axis_index("line") * grad_rows, grad_rows, 0
    ).astype(jnp.float32)
    gradient = (cost_quad[None, :] * own_generation + pushed).astype(jnp.bfloat16)
    return (gradient, outflow, outage_sens)


def solution(mesh):
    placed = (
        P(None, "bus"),
        P(None, "bus"),
        P(),
        P("line", "bus"),
        P("line", None),
        P("line"),
        P("line"),
        P(),
        P("bus"),
    )
    return jax.shard_map(
        on_device,
        mesh=mesh,
        in_specs=placed,
        out_specs=(P("line", "bus"), P("bus", None), P("bus", None)),
        check_vma=False,
    )
```

```python
import math

import jax
import jax.numpy as jnp
from jax import lax
from jax.experimental import pallas as pl
from jax.sharding import Mesh, PartitionSpec as P

sharpness = 4.0
BUS = ("y", "zh")
LINE = ("zl", "x", "core")


def penalty_slopes(base, outflow, lodf, limits):
    scen_rows, monitor_count = base.shape
    outage_total = outflow.shape[1]
    sb = 8
    ch = 16
    lanes = 128
    blocks = scen_rows // sb
    half = sharpness / 2
    base3 = (half * base).reshape(blocks, sb, monitor_count).transpose(0, 2, 1)
    lodf2 = half * lodf
    lim2 = (half * limits).reshape(monitor_count, 1)

    def kernel(base_ref, out_ref, lodf_ref, lim_ref, direct_ref, sens_ref):
        for i in range(sb):
            flow_row = out_ref[i:i + 1, :]

            def body(c, acc):
                r = pl.multiple_of(c * ch, ch)
                weight = lodf_ref[pl.ds(r, ch), :]
                bound = lim_ref[pl.ds(r, ch), :]
                post = base_ref[pl.ds(r, ch), i:i + 1] + weight * flow_row
                slope = jnp.tanh(post - bound) + jnp.tanh(post + bound)
                folded = slope[:, 0:lanes]
                for q in range(1, outage_total // lanes):
                    folded = folded + slope[:, q * lanes:(q + 1) * lanes]
                direct_ref[i, pl.ds(r, ch), :] = folded
                return acc + weight * slope

            acc = lax.fori_loop(0, monitor_count // ch, body,
                                jnp.zeros((ch, outage_total), jnp.float32),
                                unroll=monitor_count // ch)
            sens_ref[i:i + 1, :] = jnp.sum(acc, axis=0, keepdims=True)

    direct_lanes, sens = pl.pallas_call(
        kernel,
        grid=(blocks,),
        in_specs=[
            pl.BlockSpec((None, monitor_count, sb), lambda g: (g, 0, 0)),
            pl.BlockSpec((sb, outage_total), lambda g: (g, 0)),
            pl.BlockSpec((monitor_count, outage_total), lambda g: (0, 0)),
            pl.BlockSpec((monitor_count, 1), lambda g: (0, 0)),
        ],
        out_specs=[
            pl.BlockSpec((sb, monitor_count, lanes), lambda g: (g, 0, 0)),
            pl.BlockSpec((sb, outage_total), lambda g: (g, 0)),
        ],
        out_shape=[
            jax.ShapeDtypeStruct((scen_rows, monitor_count, lanes), jnp.float32),
            jax.ShapeDtypeStruct((scen_rows, outage_total), jnp.float32),
        ],
    )(base3, outflow, lodf2, lim2)
    direct = jnp.sum(direct_lanes, axis=2) / (2.0 * outage_total)
    return direct, sens / (2.0 * half)


def exchange_sum(values, axis, count):
    blocks = values.reshape((count, values.shape[0] // count) + values.shape[1:])
    return jnp.sum(lax.all_to_all(blocks, axis, 0, 0, tiled=False), axis=0)


def gather_columns(values, axis, count):
    copies = jnp.broadcast_to(values[None], (count,) + values.shape)
    gathered = lax.all_to_all(copies, axis, 0, 0, tiled=False)
    return gathered.transpose(1, 0, 2).reshape(values.shape[0], count * values.shape[1])


def gather_rows(values, axis):
    count = lax.axis_size(axis)
    copies = jnp.broadcast_to(values[None], (count,) + values.shape)
    gathered = lax.all_to_all(copies, axis, 0, 0, tiled=False)
    return gathered.reshape((count * values.shape[0],) + values.shape[1:])


def line_index():
    index = lax.axis_index(LINE[0])
    for name in LINE[1:]:
        index = index * lax.axis_size(name) + lax.axis_index(name)
    return index


def on_device(
    generation, profiles, scen_profile, ptdf, lodf, limits, monitored, outages, cost_quad
):
    line_count = lax.axis_size(LINE)
    profile_count = profiles.shape[0]
    profile_pick = (
        scen_profile[:, None] == jnp.arange(profile_count, dtype=jnp.int32)[None, :]
    ).astype(jnp.float32)
    loads = jnp.dot(profile_pick, profiles, precision=lax.Precision.HIGHEST)
    injection = (generation.astype(jnp.float32) - loads).astype(jnp.bfloat16)
    scen_rows = injection.shape[0] // lax.axis_size(BUS)
    line_rows = ptdf.shape[0]
    first_line = line_index() * line_rows
    local_monitored = monitored - first_line
    monitor_count = monitored.shape[0]
    outage_total = outages.shape[0]
    monitored_total = monitor_count * line_count

    rel_outages = outages - first_line
    in_block = (rel_outages >= 0) & (rel_outages < line_rows)
    outage_rows = jnp.where(
        in_block[:, None],
        jnp.take(ptdf, jnp.clip(rel_outages, 0, line_rows - 1), axis=0),
        jnp.zeros((), ptdf.dtype),
    )
    my_outage_rows = exchange_sum(outage_rows, LINE, line_count)
    monitored_rows = jnp.take(ptdf, local_monitored, axis=0)
    rows = jnp.concatenate([monitored_rows, my_outage_rows], axis=0)

    flow_part = lax.dot_general(
        injection, rows, (((1,), (1,)), ((), ())), preferred_element_type=jnp.float32
    )
    flow_field = exchange_sum(
        exchange_sum(flow_part, "y", lax.axis_size("y")), "zh", lax.axis_size("zh")
    )
    base = flow_field[:, :monitor_count]
    outflow = gather_columns(flow_field[:, monitor_count:], LINE, line_count)

    direct, sens_part = penalty_slopes(base, outflow, lodf, limits)

    matches = (outages[:, None] == monitored[None, :]).astype(jnp.float32)
    flag_part = jnp.sum(matches, axis=1)
    extended = jnp.concatenate(
        [sens_part, flag_part[None, :], jnp.zeros((7, outage_total), jnp.float32)], axis=0
    )
    out_share = outage_total // line_count
    shares = extended.reshape(extended.shape[0], line_count, out_share).transpose(1, 0, 2)
    mine = jnp.sum(lax.all_to_all(shares, LINE, 0, 0, tiled=False), axis=0)
    sens_mine = mine[:scen_rows]
    flag_mine = mine[scen_rows]
    sens_total = gather_columns(sens_mine, LINE, line_count)
    backward = sens_total / outage_total
    outage_sens = sens_total / math.sqrt(monitored_total)

    adjoint_monitored = (
        direct + jnp.dot(backward, matches, precision=lax.Precision.HIGHEST)
    ).astype(jnp.bfloat16)
    adjoint_outage = jnp.where(
        flag_mine[None, :] > 0.5, 0.0, sens_mine / outage_total
    ).astype(jnp.bfloat16)
    piece = jnp.concatenate([adjoint_monitored, adjoint_outage], axis=1)
    all_piece = gather_rows(gather_rows(piece, "zh"), "y")
    grad_rows = all_piece.shape[0] // line_count
    pushed = exchange_sum(
        jnp.dot(all_piece, rows, preferred_element_type=jnp.float32), LINE, line_count
    )
    own_generation = lax.dynamic_slice_in_dim(
        generation, line_index() * grad_rows, grad_rows, 0
    ).astype(jnp.float32)
    gradient = (cost_quad[None, :] * own_generation + pushed).astype(jnp.bfloat16)
    return (gradient, outflow, outage_sens)


def solution(mesh):
    fine = Mesh(mesh.devices.reshape(4, 4, 2, 4, 2), BUS + LINE)
    placed = (
        P(None, BUS),
        P(None, BUS),
        P(),
        P(LINE, BUS),
        P(LINE, None),
        P(LINE),
        P(LINE),
        P(),
        P(BUS),
    )
    return jax.shard_map(
        on_device,
        mesh=fine,
        in_specs=placed,
        out_specs=(P(LINE, BUS), P(BUS, None), P(BUS, None)),
        check_vma=False,
    )
```

```python
import math

import jax
import jax.numpy as jnp
from jax import lax
from jax.experimental import pallas as pl
from jax.sharding import Mesh, PartitionSpec as P

sharpness = 4.0
BUS = ("y", "zh")
LINE = ("zl", "x", "core")


def penalty_slopes(base, outflow, lodf, limits):
    scen_rows, monitor_count = base.shape
    outage_total = outflow.shape[1]
    sb = 8
    ch = 16
    lanes = 128
    blocks = scen_rows // sb
    half = sharpness / 2
    base3 = (half * base).reshape(blocks, sb, monitor_count).transpose(0, 2, 1)
    lodf2 = half * lodf
    lim2 = (half * limits).reshape(monitor_count, 1)

    def kernel(base_ref, out_ref, lodf_ref, lim_ref, direct_ref, sens_ref):
        for i in range(sb):
            flow_row = out_ref[i:i + 1, :]

            def body(c, acc):
                r = pl.multiple_of(c * ch, ch)
                weight = lodf_ref[pl.ds(r, ch), :]
                bound = lim_ref[pl.ds(r, ch), :]
                post = base_ref[pl.ds(r, ch), i:i + 1] + weight * flow_row
                slope = jnp.tanh(post - bound) + jnp.tanh(post + bound)
                folded = slope[:, 0:lanes]
                for q in range(1, outage_total // lanes):
                    folded = folded + slope[:, q * lanes:(q + 1) * lanes]
                direct_ref[i, pl.ds(r, ch), :] = folded
                return acc + weight * slope

            acc = lax.fori_loop(0, monitor_count // ch, body,
                                jnp.zeros((ch, outage_total), jnp.float32),
                                unroll=monitor_count // ch)
            sens_ref[i:i + 1, :] = jnp.sum(acc, axis=0, keepdims=True)

    direct_lanes, sens = pl.pallas_call(
        kernel,
        grid=(blocks,),
        in_specs=[
            pl.BlockSpec((None, monitor_count, sb), lambda g: (g, 0, 0)),
            pl.BlockSpec((sb, outage_total), lambda g: (g, 0)),
            pl.BlockSpec((monitor_count, outage_total), lambda g: (0, 0)),
            pl.BlockSpec((monitor_count, 1), lambda g: (0, 0)),
        ],
        out_specs=[
            pl.BlockSpec((sb, monitor_count, lanes), lambda g: (g, 0, 0)),
            pl.BlockSpec((sb, outage_total), lambda g: (g, 0)),
        ],
        out_shape=[
            jax.ShapeDtypeStruct((scen_rows, monitor_count, lanes), jnp.float32),
            jax.ShapeDtypeStruct((scen_rows, outage_total), jnp.float32),
        ],
    )(base3, outflow, lodf2, lim2)
    direct = jnp.sum(direct_lanes, axis=2) / (2.0 * outage_total)
    return direct, sens / (2.0 * half)


def exchange_sum(values, axis, count):
    blocks = values.reshape((count, values.shape[0] // count) + values.shape[1:])
    return jnp.sum(lax.all_to_all(blocks, axis, 0, 0, tiled=False), axis=0)


def gather_columns(values, axis, count):
    copies = jnp.broadcast_to(values[None], (count,) + values.shape)
    gathered = lax.all_to_all(copies, axis, 0, 0, tiled=False)
    return gathered.transpose(1, 0, 2).reshape(values.shape[0], count * values.shape[1])


def gather_rows(values, axis):
    count = lax.axis_size(axis)
    copies = jnp.broadcast_to(values[None], (count,) + values.shape)
    gathered = lax.all_to_all(copies, axis, 0, 0, tiled=False)
    return gathered.reshape((count * values.shape[0],) + values.shape[1:])


def line_index():
    index = lax.axis_index(LINE[0])
    for name in LINE[1:]:
        index = index * lax.axis_size(name) + lax.axis_index(name)
    return index


def on_device(
    generation, profiles, scen_profile, ptdf, lodf, limits, monitored, outages, cost_quad
):
    line_count = lax.axis_size(LINE)
    profile_count = profiles.shape[0]
    profile_pick = (
        scen_profile[:, None] == jnp.arange(profile_count, dtype=jnp.int32)[None, :]
    ).astype(jnp.float32)
    loads = jnp.dot(profile_pick, profiles, precision=lax.Precision.HIGHEST)
    injection = (generation.astype(jnp.float32) - loads).astype(jnp.bfloat16)
    scen_rows = injection.shape[0] // lax.axis_size(BUS)
    line_rows = ptdf.shape[0]
    first_line = line_index() * line_rows
    local_monitored = monitored - first_line
    monitor_count = monitored.shape[0]
    outage_total = outages.shape[0]
    monitored_total = monitor_count * line_count

    rel_outages = outages - first_line
    in_block = (rel_outages >= 0) & (rel_outages < line_rows)
    outage_rows = jnp.where(
        in_block[:, None],
        jnp.take(ptdf, jnp.clip(rel_outages, 0, line_rows - 1), axis=0),
        jnp.zeros((), ptdf.dtype),
    )
    my_outage_rows = exchange_sum(outage_rows, LINE, line_count)
    monitored_rows = jnp.take(ptdf, local_monitored, axis=0)
    rows = jnp.concatenate([monitored_rows, my_outage_rows], axis=0)

    flow_part = lax.dot_general(
        injection, rows, (((1,), (1,)), ((), ())), preferred_element_type=jnp.float32
    )
    flow_field = exchange_sum(
        exchange_sum(flow_part, "y", lax.axis_size("y")), "zh", lax.axis_size("zh")
    )
    base = flow_field[:, :monitor_count]
    outflow = gather_columns(flow_field[:, monitor_count:], LINE, line_count)

    direct, sens_part = penalty_slopes(base, outflow, lodf, limits)

    matches = (outages[:, None] == monitored[None, :]).astype(jnp.float32)
    flag_part = jnp.sum(matches, axis=1)
    extended = jnp.concatenate(
        [sens_part, flag_part[None, :], jnp.zeros((7, outage_total), jnp.float32)], axis=0
    )
    out_share = outage_total // line_count
    shares = extended.reshape(extended.shape[0], line_count, out_share).transpose(1, 0, 2)
    mine = jnp.sum(lax.all_to_all(shares, LINE, 0, 0, tiled=False), axis=0)
    sens_mine = mine[:scen_rows]
    flag_mine = mine[scen_rows]
    sens_total = gather_columns(sens_mine, LINE, line_count)
    backward = sens_total / outage_total
    outage_sens = sens_total / math.sqrt(monitored_total)

    adjoint_monitored = (
        direct + jnp.dot(backward, matches, precision=lax.Precision.HIGHEST)
    ).astype(jnp.bfloat16)
    adjoint_outage = jnp.where(
        flag_mine[None, :] > 0.5, 0.0, sens_mine / outage_total
    ).astype(jnp.bfloat16)
    piece = jnp.concatenate([adjoint_monitored, adjoint_outage], axis=1)
    all_piece = gather_rows(gather_rows(piece, "zh"), "y")
    grad_rows = all_piece.shape[0] // line_count
    staged_order = [lax.axis_size(name) for name in LINE]
    ordered_piece = (
        all_piece.reshape(staged_order + [grad_rows, all_piece.shape[1]])
        .transpose(2, 1, 0, 3, 4)
        .reshape(all_piece.shape)
    )
    pushed = jnp.dot(ordered_piece, rows, preferred_element_type=jnp.float32)
    for name in LINE[::-1]:
        pushed = exchange_sum(pushed, name, lax.axis_size(name))
    own_generation = lax.dynamic_slice_in_dim(
        generation, line_index() * grad_rows, grad_rows, 0
    ).astype(jnp.float32)
    gradient = (cost_quad[None, :] * own_generation + pushed).astype(jnp.bfloat16)
    return (gradient, outflow, outage_sens)


def solution(mesh):
    fine = Mesh(mesh.devices.reshape(4, 4, 2, 4, 2), BUS + LINE)
    placed = (
        P(None, BUS),
        P(None, BUS),
        P(),
        P(LINE, BUS),
        P(LINE, None),
        P(LINE),
        P(LINE),
        P(),
        P(BUS),
    )
    return jax.shard_map(
        on_device,
        mesh=fine,
        in_specs=placed,
        out_specs=(P(LINE, BUS), P(BUS, None), P(BUS, None)),
        check_vma=False,
    )
```

```python
import math

import jax
import jax.numpy as jnp
from jax import lax
from jax.experimental import pallas as pl
from jax.experimental.pallas import tpu as pltpu
from jax.sharding import Mesh, PartitionSpec as P

sharpness = 4.0
BUS = ("y", "zh")
LINE = ("zl", "x", "core")


def penalty_slopes(base, outflow, lodf, limits):
    scen_rows, monitor_count = base.shape
    outage_total = outflow.shape[1]
    sb = 8
    ch = 16
    lanes = 128
    blocks = scen_rows // sb
    half = sharpness / 2
    base3 = (half * base).reshape(blocks, sb, monitor_count).transpose(0, 2, 1)
    lodf2 = half * lodf
    lim2 = (half * limits).reshape(monitor_count, 1)

    def kernel(base_ref, out_ref, lodf_ref, lim_ref, direct_ref, sens_ref, fold_ref):
        for i in range(sb):
            flow_row = out_ref[i:i + 1, :]

            def body(c, acc):
                r = pl.multiple_of(c * ch, ch)
                weight = lodf_ref[pl.ds(r, ch), :]
                bound = lim_ref[pl.ds(r, ch), :]
                post = base_ref[pl.ds(r, ch), i:i + 1] + weight * flow_row
                slope = jnp.tanh(post - bound) + jnp.tanh(post + bound)
                folded = slope[:, 0:lanes]
                for q in range(1, outage_total // lanes):
                    folded = folded + slope[:, q * lanes:(q + 1) * lanes]
                fold_ref[pl.ds(r, ch), :] = folded
                return acc + weight * slope

            acc = lax.fori_loop(0, monitor_count // ch, body,
                                jnp.zeros((ch, outage_total), jnp.float32),
                                unroll=monitor_count // ch)
            sens_ref[i:i + 1, :] = jnp.sum(acc, axis=0, keepdims=True)
            direct_ref[:, i:i + 1] = jnp.sum(fold_ref[...], axis=1, keepdims=True)

    direct3, sens = pl.pallas_call(
        kernel,
        grid=(blocks,),
        in_specs=[
            pl.BlockSpec((None, monitor_count, sb), lambda g: (g, 0, 0)),
            pl.BlockSpec((sb, outage_total), lambda g: (g, 0)),
            pl.BlockSpec((monitor_count, outage_total), lambda g: (0, 0)),
            pl.BlockSpec((monitor_count, 1), lambda g: (0, 0)),
        ],
        out_specs=[
            pl.BlockSpec((None, monitor_count, sb), lambda g: (g, 0, 0)),
            pl.BlockSpec((sb, outage_total), lambda g: (g, 0)),
        ],
        out_shape=[
            jax.ShapeDtypeStruct((blocks, monitor_count, sb), jnp.float32),
            jax.ShapeDtypeStruct((scen_rows, outage_total), jnp.float32),
        ],
        scratch_shapes=[pltpu.VMEM((monitor_count, lanes), jnp.float32)],
    )(base3, outflow, lodf2, lim2)
    direct = direct3.transpose(0, 2, 1).reshape(scen_rows, monitor_count) / (2.0 * outage_total)
    return direct, sens / (2.0 * half)


def exchange_sum(values, axis, count):
    blocks = values.reshape((count, values.shape[0] // count) + values.shape[1:])
    return jnp.sum(lax.all_to_all(blocks, axis, 0, 0, tiled=False), axis=0)


def gather_columns(values, axis, count):
    copies = jnp.broadcast_to(values[None], (count,) + values.shape)
    gathered = lax.all_to_all(copies, axis, 0, 0, tiled=False)
    return gathered.transpose(1, 0, 2).reshape(values.shape[0], count * values.shape[1])


def gather_rows(values, axis):
    count = lax.axis_size(axis)
    copies = jnp.broadcast_to(values[None], (count,) + values.shape)
    gathered = lax.all_to_all(copies, axis, 0, 0, tiled=False)
    return gathered.reshape((count * values.shape[0],) + values.shape[1:])


def line_index():
    index = lax.axis_index(LINE[0])
    for name in LINE[1:]:
        index = index * lax.axis_size(name) + lax.axis_index(name)
    return index


def on_device(
    generation, profiles, scen_profile, ptdf, lodf, limits, monitored, outages, cost_quad
):
    line_count = lax.axis_size(LINE)
    profile_count = profiles.shape[0]
    profile_pick = (
        scen_profile[:, None] == jnp.arange(profile_count, dtype=jnp.int32)[None, :]
    ).astype(jnp.float32)
    loads = jnp.dot(profile_pick, profiles, precision=lax.Precision.HIGHEST)
    injection = (generation.astype(jnp.float32) - loads).astype(jnp.bfloat16)
    scen_rows = injection.shape[0] // lax.axis_size(BUS)
    line_rows = ptdf.shape[0]
    first_line = line_index() * line_rows
    local_monitored = monitored - first_line
    monitor_count = monitored.shape[0]
    outage_total = outages.shape[0]
    monitored_total = monitor_count * line_count

    rel_outages = outages - first_line
    in_block = (rel_outages >= 0) & (rel_outages < line_rows)
    outage_rows = jnp.where(
        in_block[:, None],
        jnp.take(ptdf, jnp.clip(rel_outages, 0, line_rows - 1), axis=0),
        jnp.zeros((), ptdf.dtype),
    )
    my_outage_rows = exchange_sum(outage_rows, LINE, line_count)
    monitored_rows = jnp.take(ptdf, local_monitored, axis=0)
    rows = jnp.concatenate([monitored_rows, my_outage_rows], axis=0)

    flow_part = lax.dot_general(
        injection, rows, (((1,), (1,)), ((), ())), preferred_element_type=jnp.float32
    )
    flow_field = exchange_sum(
        exchange_sum(flow_part, "y", lax.axis_size("y")), "zh", lax.axis_size("zh")
    )
    base = flow_field[:, :monitor_count]
    outflow = gather_columns(flow_field[:, monitor_count:], LINE, line_count)

    direct, sens_part = penalty_slopes(base, outflow, lodf, limits)

    matches = (outages[:, None] == monitored[None, :]).astype(jnp.float32)
    flag_part = jnp.sum(matches, axis=1)
    extended = jnp.concatenate(
        [sens_part, flag_part[None, :], jnp.zeros((7, outage_total), jnp.float32)], axis=0
    )
    out_share = outage_total // line_count
    shares = extended.reshape(extended.shape[0], line_count, out_share).transpose(1, 0, 2)
    mine = jnp.sum(lax.all_to_all(shares, LINE, 0, 0, tiled=False), axis=0)
    sens_mine = mine[:scen_rows]
    flag_mine = mine[scen_rows]
    sens_total = gather_columns(sens_mine, LINE, line_count)
    backward = sens_total / outage_total
    outage_sens = sens_total / math.sqrt(monitored_total)

    adjoint_monitored = (
        direct + jnp.dot(backward, matches, precision=lax.Precision.HIGHEST)
    ).astype(jnp.bfloat16)
    adjoint_outage = jnp.where(
        flag_mine[None, :] > 0.5, 0.0, sens_mine / outage_total
    ).astype(jnp.bfloat16)
    piece = jnp.concatenate([adjoint_monitored, adjoint_outage], axis=1)
    all_piece = gather_rows(gather_rows(piece, "zh"), "y")
    grad_rows = all_piece.shape[0] // line_count
    staged_order = [lax.axis_size(name) for name in LINE]
    ordered_piece = (
        all_piece.reshape(staged_order + [grad_rows, all_piece.shape[1]])
        .transpose(2, 1, 0, 3, 4)
        .reshape(all_piece.shape)
    )
    pushed = jnp.dot(ordered_piece, rows, preferred_element_type=jnp.float32)
    for name in LINE[::-1]:
        pushed = exchange_sum(pushed, name, lax.axis_size(name))
    own_generation = lax.dynamic_slice_in_dim(
        generation, line_index() * grad_rows, grad_rows, 0
    ).astype(jnp.float32)
    gradient = (cost_quad[None, :] * own_generation + pushed).astype(jnp.bfloat16)
    return (gradient, outflow, outage_sens)


def solution(mesh):
    fine = Mesh(mesh.devices.reshape(4, 4, 2, 4, 2), BUS + LINE)
    placed = (
        P(None, BUS),
        P(None, BUS),
        P(),
        P(LINE, BUS),
        P(LINE, None),
        P(LINE),
        P(LINE),
        P(),
        P(BUS),
    )
    return jax.shard_map(
        on_device,
        mesh=fine,
        in_specs=placed,
        out_specs=(P(LINE, BUS), P(BUS, None), P(BUS, None)),
        check_vma=False,
    )
```

```python
import math

import jax
import jax.numpy as jnp
from jax import lax
from jax.experimental import pallas as pl
from jax.sharding import Mesh, PartitionSpec as P

sharpness = 4.0
BUS = ("y", "zh")
LINE = ("zl", "x", "core")


def penalty_slopes(base, outflow, lodf, limits):
    scen_rows, monitor_count = base.shape
    outage_total = outflow.shape[1]
    sb = 8
    ch = 16
    lanes = 128
    blocks = scen_rows // sb
    half = sharpness / 2
    base3 = (half * base).reshape(blocks, sb, monitor_count).transpose(0, 2, 1)
    lodf2 = half * lodf
    lim2 = (half * limits).reshape(monitor_count, 1)

    def kernel(base_ref, out_ref, lodf_ref, lim_ref, direct_ref, sens_ref):
        for i in range(sb):
            flow_row = out_ref[i:i + 1, :]

            def body(c, acc):
                r = pl.multiple_of(c * ch, ch)
                weight = lodf_ref[pl.ds(r, ch), :]
                bound = lim_ref[pl.ds(r, ch), :]
                post = base_ref[pl.ds(r, ch), i:i + 1] + weight * flow_row
                slope = jnp.tanh(post - bound) + jnp.tanh(post + bound)
                folded = slope[:, 0:lanes]
                for q in range(1, outage_total // lanes):
                    folded = folded + slope[:, q * lanes:(q + 1) * lanes]
                direct_ref[i, pl.ds(r, ch), :] = folded
                return acc + weight * slope

            acc = lax.fori_loop(0, monitor_count // ch, body,
                                jnp.zeros((ch, outage_total), jnp.float32),
                                unroll=monitor_count // ch)
            sens_ref[i:i + 1, :] = jnp.sum(acc, axis=0, keepdims=True)

    direct_lanes, sens = pl.pallas_call(
        kernel,
        grid=(blocks,),
        in_specs=[
            pl.BlockSpec((None, monitor_count, sb), lambda g: (g, 0, 0)),
            pl.BlockSpec((sb, outage_total), lambda g: (g, 0)),
            pl.BlockSpec((monitor_count, outage_total), lambda g: (0, 0)),
            pl.BlockSpec((monitor_count, 1), lambda g: (0, 0)),
        ],
        out_specs=[
            pl.BlockSpec((sb, monitor_count, lanes), lambda g: (g, 0, 0)),
            pl.BlockSpec((sb, outage_total), lambda g: (g, 0)),
        ],
        out_shape=[
            jax.ShapeDtypeStruct((scen_rows, monitor_count, lanes), jnp.float32),
            jax.ShapeDtypeStruct((scen_rows, outage_total), jnp.float32),
        ],
    )(base3, outflow, lodf2, lim2)
    direct = jnp.sum(direct_lanes, axis=2) / (2.0 * outage_total)
    return direct, sens / (2.0 * half)


def exchange_sum(values, axis, count):
    blocks = values.reshape((count, values.shape[0] // count) + values.shape[1:])
    return jnp.sum(lax.all_to_all(blocks, axis, 0, 0, tiled=False), axis=0)


def gather_columns(values, axis, count):
    copies = jnp.broadcast_to(values[None], (count,) + values.shape)
    gathered = lax.all_to_all(copies, axis, 0, 0, tiled=False)
    return gathered.transpose(1, 0, 2).reshape(values.shape[0], count * values.shape[1])


def gather_rows(values, axis):
    count = lax.axis_size(axis)
    copies = jnp.broadcast_to(values[None], (count,) + values.shape)
    gathered = lax.all_to_all(copies, axis, 0, 0, tiled=False)
    return gathered.reshape((count * values.shape[0],) + values.shape[1:])


def line_index():
    index = lax.axis_index(LINE[0])
    for name in LINE[1:]:
        index = index * lax.axis_size(name) + lax.axis_index(name)
    return index


def on_device(
    generation, profiles, scen_profile, ptdf, lodf, limits, monitored, outages, cost_quad
):
    line_count = lax.axis_size(LINE)
    profile_count = profiles.shape[0]
    profile_pick = (
        scen_profile[:, None] == jnp.arange(profile_count, dtype=jnp.int32)[None, :]
    ).astype(jnp.float32)
    loads = jnp.dot(profile_pick, profiles, precision=lax.Precision.HIGHEST)
    injection = (generation.astype(jnp.float32) - loads).astype(jnp.bfloat16)
    scen_rows = injection.shape[0] // lax.axis_size(BUS)
    line_rows = ptdf.shape[0]
    first_line = line_index() * line_rows
    local_monitored = monitored - first_line
    monitor_count = monitored.shape[0]
    outage_total = outages.shape[0]
    monitored_total = monitor_count * line_count

    rel_outages = outages - first_line
    in_block = (rel_outages >= 0) & (rel_outages < line_rows)
    outage_rows = jnp.where(
        in_block[:, None],
        jnp.take(ptdf, jnp.clip(rel_outages, 0, line_rows - 1), axis=0),
        jnp.zeros((), ptdf.dtype),
    )
    my_outage_rows = exchange_sum(outage_rows, LINE, line_count)
    monitored_rows = jnp.take(ptdf, local_monitored, axis=0)
    rows = jnp.concatenate([monitored_rows, my_outage_rows], axis=0)

    flow_part = lax.dot_general(
        injection, rows, (((1,), (1,)), ((), ())), preferred_element_type=jnp.float32
    )
    flow_field = exchange_sum(
        exchange_sum(flow_part, "y", lax.axis_size("y")), "zh", lax.axis_size("zh")
    )
    base = flow_field[:, :monitor_count]
    outflow = gather_columns(flow_field[:, monitor_count:], LINE, line_count)

    direct, sens_part = penalty_slopes(base, outflow, lodf, limits)

    out_share = outage_total // line_count
    shares = sens_part.reshape(scen_rows, line_count, out_share).transpose(1, 0, 2)
    sens_mine = jnp.sum(lax.all_to_all(shares, LINE, 0, 0, tiled=False), axis=0)
    sens_total = gather_columns(sens_mine, LINE, line_count)
    outage_sens = sens_total / math.sqrt(monitored_total)

    adjoint_monitored = direct.astype(jnp.bfloat16)
    adjoint_outage = (sens_mine / outage_total).astype(jnp.bfloat16)
    piece = jnp.concatenate([adjoint_monitored, adjoint_outage], axis=1)
    all_piece = gather_rows(gather_rows(piece, "zh"), "y")
    grad_rows = all_piece.shape[0] // line_count
    staged_order = [lax.axis_size(name) for name in LINE]
    ordered_piece = (
        all_piece.reshape(staged_order + [grad_rows, all_piece.shape[1]])
        .transpose(2, 1, 0, 3, 4)
        .reshape(all_piece.shape)
    )
    pushed = jnp.dot(ordered_piece, rows, preferred_element_type=jnp.float32)
    for name in LINE[::-1]:
        pushed = exchange_sum(pushed, name, lax.axis_size(name))
    own_generation = lax.dynamic_slice_in_dim(
        generation, line_index() * grad_rows, grad_rows, 0
    ).astype(jnp.float32)
    gradient = (cost_quad[None, :] * own_generation + pushed).astype(jnp.bfloat16)
    return (gradient, outflow, outage_sens)


def solution(mesh):
    fine = Mesh(mesh.devices.reshape(4, 4, 2, 4, 2), BUS + LINE)
    placed = (
        P(None, BUS),
        P(None, BUS),
        P(),
        P(LINE, BUS),
        P(LINE, None),
        P(LINE),
        P(LINE),
        P(),
        P(BUS),
    )
    return jax.shard_map(
        on_device,
        mesh=fine,
        in_specs=placed,
        out_specs=(P(LINE, BUS), P(BUS, None), P(BUS, None)),
        check_vma=False,
    )
```

```python
import math

import jax
import jax.numpy as jnp
from jax import lax
from jax.experimental import pallas as pl
from jax.sharding import Mesh, PartitionSpec as P

sharpness = 4.0
BUS = ("y", "zh")
LINE = ("zl", "x", "core")


def penalty_slopes(base, outflow, lodf, limits):
    scen_rows, monitor_count = base.shape
    outage_total = outflow.shape[1]
    sb = 8
    ch = 16
    lanes = 128
    blocks = scen_rows // sb
    half = sharpness / 2
    base3 = (half * base).reshape(blocks, sb, monitor_count).transpose(0, 2, 1)
    lodf2 = half * lodf
    lim2 = (half * limits).reshape(monitor_count, 1)

    def kernel(base_ref, out_ref, lodf_ref, lim_ref, direct_ref, sens_ref):
        for i in range(sb):
            flow_row = out_ref[i:i + 1, :]

            def body(c, acc):
                r = pl.multiple_of(c * ch, ch)
                weight = lodf_ref[pl.ds(r, ch), :]
                bound = lim_ref[pl.ds(r, ch), :]
                post = base_ref[pl.ds(r, ch), i:i + 1] + weight * flow_row
                slope = jnp.tanh(post - bound) + jnp.tanh(post + bound)
                folded = slope[:, 0:lanes]
                for q in range(1, outage_total // lanes):
                    folded = folded + slope[:, q * lanes:(q + 1) * lanes]
                direct_ref[i, pl.ds(r, ch), :] = folded
                return acc + weight * slope

            acc = lax.fori_loop(0, monitor_count // ch, body,
                                jnp.zeros((ch, outage_total), jnp.float32),
                                unroll=monitor_count // ch)
            sens_ref[i:i + 1, :] = jnp.sum(acc, axis=0, keepdims=True)

    direct_lanes, sens = pl.pallas_call(
        kernel,
        grid=(blocks,),
        in_specs=[
            pl.BlockSpec((None, monitor_count, sb), lambda g: (g, 0, 0)),
            pl.BlockSpec((sb, outage_total), lambda g: (g, 0)),
            pl.BlockSpec((monitor_count, outage_total), lambda g: (0, 0)),
            pl.BlockSpec((monitor_count, 1), lambda g: (0, 0)),
        ],
        out_specs=[
            pl.BlockSpec((sb, monitor_count, lanes), lambda g: (g, 0, 0)),
            pl.BlockSpec((sb, outage_total), lambda g: (g, 0)),
        ],
        out_shape=[
            jax.ShapeDtypeStruct((scen_rows, monitor_count, lanes), jnp.float32),
            jax.ShapeDtypeStruct((scen_rows, outage_total), jnp.float32),
        ],
    )(base3, outflow, lodf2, lim2)
    direct = jnp.sum(direct_lanes, axis=2) / (2.0 * outage_total)
    return direct, sens / (2.0 * half)


def exchange_sum(values, axis, count):
    blocks = values.reshape((count, values.shape[0] // count) + values.shape[1:])
    return jnp.sum(lax.all_to_all(blocks, axis, 0, 0, tiled=False), axis=0)


def gather_columns(values, axis, count):
    copies = jnp.broadcast_to(values[None], (count,) + values.shape)
    gathered = lax.all_to_all(copies, axis, 0, 0, tiled=False)
    return gathered.transpose(1, 0, 2).reshape(values.shape[0], count * values.shape[1])


def gather_rows(values, axis):
    count = lax.axis_size(axis)
    copies = jnp.broadcast_to(values[None], (count,) + values.shape)
    gathered = lax.all_to_all(copies, axis, 0, 0, tiled=False)
    return gathered.reshape((count * values.shape[0],) + values.shape[1:])


def line_index():
    index = lax.axis_index(LINE[0])
    for name in LINE[1:]:
        index = index * lax.axis_size(name) + lax.axis_index(name)
    return index


def on_device(
    generation, profiles, scen_profile, ptdf, lodf, limits, monitored, outages, cost_quad
):
    line_count = lax.axis_size(LINE)
    profile_count = profiles.shape[0]
    profile_pick = (
        scen_profile[:, None] == jnp.arange(profile_count, dtype=jnp.int32)[None, :]
    ).astype(jnp.float32)
    loads = jnp.dot(profile_pick, profiles, precision=lax.Precision.HIGHEST)
    injection = (generation.astype(jnp.float32) - loads).astype(jnp.bfloat16)
    scen_rows = injection.shape[0] // lax.axis_size(BUS)
    line_rows = ptdf.shape[0]
    first_line = line_index() * line_rows
    local_monitored = monitored - first_line
    monitor_count = monitored.shape[0]
    outage_total = outages.shape[0]
    monitored_total = monitor_count * line_count

    rel_outages = outages - first_line
    in_block = (rel_outages >= 0) & (rel_outages < line_rows)
    outage_rows = jnp.where(
        in_block[:, None],
        jnp.take(ptdf, jnp.clip(rel_outages, 0, line_rows - 1), axis=0),
        jnp.zeros((), ptdf.dtype),
    )
    my_outage_rows = exchange_sum(outage_rows, LINE, line_count)
    monitored_rows = jnp.take(ptdf, local_monitored, axis=0)
    rows = jnp.concatenate([monitored_rows, my_outage_rows], axis=0)

    flow_part = lax.dot_general(
        injection, rows, (((1,), (1,)), ((), ())), preferred_element_type=jnp.float32
    )
    flow_field = exchange_sum(
        exchange_sum(flow_part, "y", lax.axis_size("y")), "zh", lax.axis_size("zh")
    )
    base = flow_field[:, :monitor_count]
    outflow = gather_columns(flow_field[:, monitor_count:], LINE, line_count)

    direct, sens_part = penalty_slopes(base, outflow, lodf, limits)

    matches = (outages[:, None] == monitored[None, :]).astype(jnp.float32)
    is_outage = jnp.sum(matches, axis=0)
    direct_at = jnp.dot(direct, matches.T, precision=lax.Precision.HIGHEST)
    out_share = outage_total // line_count
    both = jnp.concatenate([sens_part, direct_at], axis=0)
    shares = both.reshape(both.shape[0], line_count, out_share).transpose(1, 0, 2)
    mine = jnp.sum(lax.all_to_all(shares, LINE, 0, 0, tiled=False), axis=0)
    sens_mine = mine[:scen_rows]
    direct_mine = mine[scen_rows:]
    sens_total = gather_columns(sens_mine, LINE, line_count)
    outage_sens = sens_total / math.sqrt(monitored_total)

    adjoint_monitored = jnp.where(is_outage[None, :] > 0.5, 0.0, direct).astype(jnp.bfloat16)
    adjoint_outage = (direct_mine + sens_mine / outage_total).astype(jnp.bfloat16)
    piece = jnp.concatenate([adjoint_monitored, adjoint_outage], axis=1)
    all_piece = gather_rows(gather_rows(piece, "zh"), "y")
    grad_rows = all_piece.shape[0] // line_count
    staged_order = [lax.axis_size(name) for name in LINE]
    ordered_piece = (
        all_piece.reshape(staged_order + [grad_rows, all_piece.shape[1]])
        .transpose(2, 1, 0, 3, 4)
        .reshape(all_piece.shape)
    )
    pushed = jnp.dot(ordered_piece, rows, preferred_element_type=jnp.float32)
    for name in LINE[::-1]:
        pushed = exchange_sum(pushed, name, lax.axis_size(name))
    own_generation = lax.dynamic_slice_in_dim(
        generation, line_index() * grad_rows, grad_rows, 0
    ).astype(jnp.float32)
    gradient = (cost_quad[None, :] * own_generation + pushed).astype(jnp.bfloat16)
    return (gradient, outflow, outage_sens)


def solution(mesh):
    fine = Mesh(mesh.devices.reshape(4, 4, 2, 4, 2), BUS + LINE)
    placed = (
        P(None, BUS),
        P(None, BUS),
        P(),
        P(LINE, BUS),
        P(LINE, None),
        P(LINE),
        P(LINE),
        P(),
        P(BUS),
    )
    return jax.shard_map(
        on_device,
        mesh=fine,
        in_specs=placed,
        out_specs=(P(LINE, BUS), P(BUS, None), P(BUS, None)),
        check_vma=False,
    )
```

```python
import math

import jax
import jax.numpy as jnp
from jax import lax
from jax.experimental import pallas as pl
from jax.sharding import Mesh, PartitionSpec as P

sharpness = 4.0
BUS = ("y", "zh")
LINE = ("zl", "x", "core")


def penalty_slopes(base, outflow, lodf, limits):
    scen_rows, monitor_count = base.shape
    outage_total = outflow.shape[1]
    sb = 8
    ch = 16
    lanes = 128
    blocks = scen_rows // sb
    half = sharpness / 2
    base3 = (half * base).reshape(blocks, sb, monitor_count).transpose(0, 2, 1)
    lodf2 = half * lodf
    lim2 = (half * limits).reshape(monitor_count, 1)

    def kernel(base_ref, out_ref, lodf_ref, lim_ref, direct_ref, sens_ref):
        for i in range(sb):
            flow_row = out_ref[i:i + 1, :]

            def body(c, acc):
                r = pl.multiple_of(c * ch, ch)
                weight = lodf_ref[pl.ds(r, ch), :]
                bound = lim_ref[pl.ds(r, ch), :]
                post = base_ref[pl.ds(r, ch), i:i + 1] + weight * flow_row
                slope = jnp.tanh(post - bound) + jnp.tanh(post + bound)
                folded = slope[:, 0:lanes]
                for q in range(1, outage_total // lanes):
                    folded = folded + slope[:, q * lanes:(q + 1) * lanes]
                direct_ref[i, pl.ds(r, ch), :] = folded
                return acc + weight * slope

            acc = lax.fori_loop(0, monitor_count // ch, body,
                                jnp.zeros((ch, outage_total), jnp.float32),
                                unroll=monitor_count // ch)
            sens_ref[i:i + 1, :] = jnp.sum(acc, axis=0, keepdims=True)

    direct_lanes, sens = pl.pallas_call(
        kernel,
        grid=(blocks,),
        in_specs=[
            pl.BlockSpec((None, monitor_count, sb), lambda g: (g, 0, 0)),
            pl.BlockSpec((sb, outage_total), lambda g: (g, 0)),
            pl.BlockSpec((monitor_count, outage_total), lambda g: (0, 0)),
            pl.BlockSpec((monitor_count, 1), lambda g: (0, 0)),
        ],
        out_specs=[
            pl.BlockSpec((sb, monitor_count, lanes), lambda g: (g, 0, 0)),
            pl.BlockSpec((sb, outage_total), lambda g: (g, 0)),
        ],
        out_shape=[
            jax.ShapeDtypeStruct((scen_rows, monitor_count, lanes), jnp.float32),
            jax.ShapeDtypeStruct((scen_rows, outage_total), jnp.float32),
        ],
    )(base3, outflow, lodf2, lim2)
    direct = jnp.sum(direct_lanes, axis=2) / (2.0 * outage_total)
    return direct, sens / (2.0 * half)


def exchange_sum(values, axis, count):
    blocks = values.reshape((count, values.shape[0] // count) + values.shape[1:])
    return jnp.sum(lax.all_to_all(blocks, axis, 0, 0, tiled=False), axis=0)


def gather_columns(values, axis, count):
    copies = jnp.broadcast_to(values[None], (count,) + values.shape)
    gathered = lax.all_to_all(copies, axis, 0, 0, tiled=False)
    return gathered.transpose(1, 0, 2).reshape(values.shape[0], count * values.shape[1])


def gather_rows(values, axis):
    count = lax.axis_size(axis)
    copies = jnp.broadcast_to(values[None], (count,) + values.shape)
    gathered = lax.all_to_all(copies, axis, 0, 0, tiled=False)
    return gathered.reshape((count * values.shape[0],) + values.shape[1:])


def line_index():
    index = lax.axis_index(LINE[0])
    for name in LINE[1:]:
        index = index * lax.axis_size(name) + lax.axis_index(name)
    return index


def on_device(
    generation, profiles, scen_profile, ptdf, lodf, limits, monitored, outages, cost_quad
):
    line_count = lax.axis_size(LINE)
    profile_count = profiles.shape[0]
    profile_pick = (
        scen_profile[:, None] == jnp.arange(profile_count, dtype=jnp.int32)[None, :]
    ).astype(jnp.float32)
    loads = jnp.dot(profile_pick, profiles, precision=lax.Precision.HIGHEST)
    injection = (generation.astype(jnp.float32) - loads).astype(jnp.bfloat16)
    scen_rows = injection.shape[0] // lax.axis_size(BUS)
    line_rows = ptdf.shape[0]
    first_line = line_index() * line_rows
    local_monitored = monitored - first_line
    monitor_count = monitored.shape[0]
    outage_total = outages.shape[0]
    monitored_total = monitor_count * line_count

    rel_outages = outages - first_line
    in_block = (rel_outages >= 0) & (rel_outages < line_rows)
    outage_rows = jnp.where(
        in_block[:, None],
        jnp.take(ptdf, jnp.clip(rel_outages, 0, line_rows - 1), axis=0),
        jnp.zeros((), ptdf.dtype),
    )
    my_outage_rows = exchange_sum(outage_rows, LINE, line_count)
    monitored_rows = jnp.take(ptdf, local_monitored, axis=0)
    rows = jnp.concatenate([monitored_rows, my_outage_rows], axis=0)

    flow_part = lax.dot_general(
        injection, rows, (((1,), (1,)), ((), ())), preferred_element_type=jnp.float32
    )
    flow_field = exchange_sum(
        exchange_sum(flow_part, "y", lax.axis_size("y")), "zh", lax.axis_size("zh")
    )
    base = flow_field[:, :monitor_count]
    outflow = gather_columns(flow_field[:, monitor_count:], LINE, line_count)

    direct, sens_part = penalty_slopes(base, outflow, lodf, limits)

    matches = (outages[:, None] == monitored[None, :]).astype(jnp.float32)
    flag_part = jnp.sum(matches, axis=1)
    extended = jnp.concatenate(
        [sens_part, flag_part[None, :], jnp.zeros((7, outage_total), jnp.float32)], axis=0
    )
    out_share = outage_total // line_count
    shares = extended.reshape(extended.shape[0], line_count, out_share).transpose(1, 0, 2)
    mine = jnp.sum(lax.all_to_all(shares, LINE, 0, 0, tiled=False), axis=0)
    sens_mine = mine[:scen_rows]
    flag_mine = mine[scen_rows]
    sens_total = gather_columns(sens_mine, LINE, line_count)
    backward = sens_total / outage_total
    outage_sens = sens_total / math.sqrt(monitored_total)

    adjoint_monitored = (
        direct + jnp.dot(backward, matches, precision=lax.Precision.HIGHEST)
    ).astype(jnp.bfloat16)
    adjoint_outage = jnp.where(
        flag_mine[None, :] > 0.5, 0.0, sens_mine / outage_total
    ).astype(jnp.bfloat16)
    piece = jnp.concatenate([adjoint_monitored, adjoint_outage], axis=1)
    all_piece = gather_rows(gather_rows(piece, "zh"), "y")
    grad_rows = all_piece.shape[0] // line_count
    staged_order = [lax.axis_size(name) for name in LINE]
    ordered_piece = (
        all_piece.reshape(staged_order + [grad_rows, all_piece.shape[1]])
        .transpose(2, 0, 1, 3, 4)
        .reshape(all_piece.shape)
    )
    pushed = jnp.dot(ordered_piece, rows, preferred_element_type=jnp.float32)
    for name in ("core", "zl", "x"):
        pushed = exchange_sum(pushed, name, lax.axis_size(name))
    own_generation = lax.dynamic_slice_in_dim(
        generation, line_index() * grad_rows, grad_rows, 0
    ).astype(jnp.float32)
    gradient = (cost_quad[None, :] * own_generation + pushed).astype(jnp.bfloat16)
    return (gradient, outflow, outage_sens)


def solution(mesh):
    fine = Mesh(mesh.devices.reshape(4, 4, 2, 4, 2), BUS + LINE)
    placed = (
        P(None, BUS),
        P(None, BUS),
        P(),
        P(LINE, BUS),
        P(LINE, None),
        P(LINE),
        P(LINE),
        P(),
        P(BUS),
    )
    return jax.shard_map(
        on_device,
        mesh=fine,
        in_specs=placed,
        out_specs=(P(LINE, BUS), P(BUS, None), P(BUS, None)),
        check_vma=False,
    )
```

```python
import math

import jax
import jax.numpy as jnp
from jax import lax
from jax.experimental import pallas as pl
from jax.sharding import Mesh, PartitionSpec as P

sharpness = 4.0
BUS = ("y", "zh")
LINE = ("zl", "x", "core")


def penalty_slopes(base, outflow, lodf, limits):
    scen_rows, monitor_count = base.shape
    outage_total = outflow.shape[1]
    sb = 8
    ch = 16
    lanes = 128
    blocks = scen_rows // sb
    half = sharpness / 2
    base3 = (half * base).reshape(blocks, sb, monitor_count).transpose(0, 2, 1)
    lodf2 = half * lodf
    lim2 = (half * limits).reshape(monitor_count, 1)

    def kernel(base_ref, out_ref, lodf_ref, lim_ref, direct_ref, sens_ref):
        for i in range(sb):
            flow_row = out_ref[i:i + 1, :]

            def body(c, acc):
                r = pl.multiple_of(c * ch, ch)
                weight = lodf_ref[pl.ds(r, ch), :]
                bound = lim_ref[pl.ds(r, ch), :]
                post = base_ref[pl.ds(r, ch), i:i + 1] + weight * flow_row
                slope = jnp.tanh(post - bound) + jnp.tanh(post + bound)
                folded = slope[:, 0:lanes]
                for q in range(1, outage_total // lanes):
                    folded = folded + slope[:, q * lanes:(q + 1) * lanes]
                direct_ref[i, pl.ds(r, ch), :] = folded
                return acc + weight * slope

            acc = lax.fori_loop(0, monitor_count // ch, body,
                                jnp.zeros((ch, outage_total), jnp.float32),
                                unroll=monitor_count // ch)
            sens_ref[i:i + 1, :] = jnp.sum(acc, axis=0, keepdims=True)

    direct_lanes, sens = pl.pallas_call(
        kernel,
        grid=(blocks,),
        in_specs=[
            pl.BlockSpec((None, monitor_count, sb), lambda g: (g, 0, 0)),
            pl.BlockSpec((sb, outage_total), lambda g: (g, 0)),
            pl.BlockSpec((monitor_count, outage_total), lambda g: (0, 0)),
            pl.BlockSpec((monitor_count, 1), lambda g: (0, 0)),
        ],
        out_specs=[
            pl.BlockSpec((sb, monitor_count, lanes), lambda g: (g, 0, 0)),
            pl.BlockSpec((sb, outage_total), lambda g: (g, 0)),
        ],
        out_shape=[
            jax.ShapeDtypeStruct((scen_rows, monitor_count, lanes), jnp.float32),
            jax.ShapeDtypeStruct((scen_rows, outage_total), jnp.float32),
        ],
    )(base3, outflow, lodf2, lim2)
    lane_ones = jnp.ones((lanes, 1), jnp.float32)
    direct = jnp.dot(
        direct_lanes.reshape(scen_rows * monitor_count, lanes), lane_ones,
        precision=lax.Precision.HIGHEST,
    ).reshape(scen_rows, monitor_count) / (2.0 * outage_total)
    return direct, sens / (2.0 * half)


def exchange_sum(values, axis, count):
    blocks = values.reshape((count, values.shape[0] // count) + values.shape[1:])
    return jnp.sum(lax.all_to_all(blocks, axis, 0, 0, tiled=False), axis=0)


def gather_columns(values, axis, count):
    copies = jnp.broadcast_to(values[None], (count,) + values.shape)
    gathered = lax.all_to_all(copies, axis, 0, 0, tiled=False)
    return gathered.transpose(1, 0, 2).reshape(values.shape[0], count * values.shape[1])


def gather_rows(values, axis):
    count = lax.axis_size(axis)
    copies = jnp.broadcast_to(values[None], (count,) + values.shape)
    gathered = lax.all_to_all(copies, axis, 0, 0, tiled=False)
    return gathered.reshape((count * values.shape[0],) + values.shape[1:])


def line_index():
    index = lax.axis_index(LINE[0])
    for name in LINE[1:]:
        index = index * lax.axis_size(name) + lax.axis_index(name)
    return index


def on_device(
    generation, profiles, scen_profile, ptdf, lodf, limits, monitored, outages, cost_quad
):
    line_count = lax.axis_size(LINE)
    profile_count = profiles.shape[0]
    profile_pick = (
        scen_profile[:, None] == jnp.arange(profile_count, dtype=jnp.int32)[None, :]
    ).astype(jnp.float32)
    loads = jnp.dot(profile_pick, profiles, precision=lax.Precision.HIGHEST)
    injection = (generation.astype(jnp.float32) - loads).astype(jnp.bfloat16)
    scen_rows = injection.shape[0] // lax.axis_size(BUS)
    line_rows = ptdf.shape[0]
    first_line = line_index() * line_rows
    local_monitored = monitored - first_line
    monitor_count = monitored.shape[0]
    outage_total = outages.shape[0]
    monitored_total = monitor_count * line_count

    rel_outages = outages - first_line
    in_block = (rel_outages >= 0) & (rel_outages < line_rows)
    outage_rows = jnp.where(
        in_block[:, None],
        jnp.take(ptdf, jnp.clip(rel_outages, 0, line_rows - 1), axis=0),
        jnp.zeros((), ptdf.dtype),
    )
    my_outage_rows = exchange_sum(outage_rows, LINE, line_count)
    monitored_rows = jnp.take(ptdf, local_monitored, axis=0)
    rows = jnp.concatenate([monitored_rows, my_outage_rows], axis=0)

    flow_part = lax.dot_general(
        injection, rows, (((1,), (1,)), ((), ())), preferred_element_type=jnp.float32
    )
    flow_field = exchange_sum(
        exchange_sum(flow_part, "y", lax.axis_size("y")), "zh", lax.axis_size("zh")
    )
    base = flow_field[:, :monitor_count]
    outflow = gather_columns(flow_field[:, monitor_count:], LINE, line_count)

    direct, sens_part = penalty_slopes(base, outflow, lodf, limits)

    matches = (outages[:, None] == monitored[None, :]).astype(jnp.float32)
    flag_part = jnp.sum(matches, axis=1)
    extended = jnp.concatenate(
        [sens_part, flag_part[None, :], jnp.zeros((7, outage_total), jnp.float32)], axis=0
    )
    out_share = outage_total // line_count
    shares = extended.reshape(extended.shape[0], line_count, out_share).transpose(1, 0, 2)
    mine = jnp.sum(lax.all_to_all(shares, LINE, 0, 0, tiled=False), axis=0)
    sens_mine = mine[:scen_rows]
    flag_mine = mine[scen_rows]
    sens_total = gather_columns(sens_mine, LINE, line_count)
    backward = sens_total / outage_total
    outage_sens = sens_total / math.sqrt(monitored_total)

    adjoint_monitored = (
        direct + jnp.dot(backward, matches, precision=lax.Precision.HIGHEST)
    ).astype(jnp.bfloat16)
    adjoint_outage = jnp.where(
        flag_mine[None, :] > 0.5, 0.0, sens_mine / outage_total
    ).astype(jnp.bfloat16)
    piece = jnp.concatenate([adjoint_monitored, adjoint_outage], axis=1)
    all_piece = gather_rows(gather_rows(piece, "zh"), "y")
    grad_rows = all_piece.shape[0] // line_count
    staged_order = [lax.axis_size(name) for name in LINE]
    ordered_piece = (
        all_piece.reshape(staged_order + [grad_rows, all_piece.shape[1]])
        .transpose(2, 1, 0, 3, 4)
        .reshape(all_piece.shape)
    )
    pushed = jnp.dot(ordered_piece, rows, preferred_element_type=jnp.float32)
    for name in LINE[::-1]:
        pushed = exchange_sum(pushed, name, lax.axis_size(name))
    own_generation = lax.dynamic_slice_in_dim(
        generation, line_index() * grad_rows, grad_rows, 0
    ).astype(jnp.float32)
    gradient = (cost_quad[None, :] * own_generation + pushed).astype(jnp.bfloat16)
    return (gradient, outflow, outage_sens)


def solution(mesh):
    fine = Mesh(mesh.devices.reshape(4, 4, 2, 4, 2), BUS + LINE)
    placed = (
        P(None, BUS),
        P(None, BUS),
        P(),
        P(LINE, BUS),
        P(LINE, None),
        P(LINE),
        P(LINE),
        P(),
        P(BUS),
    )
    return jax.shard_map(
        on_device,
        mesh=fine,
        in_specs=placed,
        out_specs=(P(LINE, BUS), P(BUS, None), P(BUS, None)),
        check_vma=False,
    )
```

```python
import math

import jax
import jax.numpy as jnp
from jax import lax
from jax.experimental import pallas as pl
from jax.sharding import Mesh, PartitionSpec as P

sharpness = 4.0
BUS = ("y", "zh")
LINE = ("zl", "x", "core")


def penalty_slopes(base, outflow, lodf, limits):
    scen_rows, monitor_count = base.shape
    outage_total = outflow.shape[1]
    sb = 8
    ch = 16
    lanes = 128
    blocks = scen_rows // sb
    half = sharpness / 2
    base3 = (half * base).reshape(blocks, sb, monitor_count).transpose(0, 2, 1)
    lodf2 = half * lodf
    lim2 = (half * limits).reshape(monitor_count, 1)

    def kernel(base_ref, out_ref, lodf_ref, lim_ref, direct_ref, sens_ref):
        for i in range(sb):
            flow_row = out_ref[i:i + 1, :]

            def body(c, acc):
                r = pl.multiple_of(c * ch, ch)
                weight = lodf_ref[pl.ds(r, ch), :]
                bound = lim_ref[pl.ds(r, ch), :]
                post = base_ref[pl.ds(r, ch), i:i + 1] + weight * flow_row
                slope = jnp.tanh(post - bound) + jnp.tanh(post + bound)
                folded = slope[:, 0:lanes]
                for q in range(1, outage_total // lanes):
                    folded = folded + slope[:, q * lanes:(q + 1) * lanes]
                direct_ref[i, pl.ds(r, ch), :] = folded
                return acc + weight * slope

            acc = lax.fori_loop(0, monitor_count // ch, body,
                                jnp.zeros((ch, outage_total), jnp.float32),
                                unroll=monitor_count // ch)
            sens_ref[i:i + 1, :] = jnp.sum(acc, axis=0, keepdims=True)

    direct_lanes, sens = pl.pallas_call(
        kernel,
        grid=(blocks,),
        in_specs=[
            pl.BlockSpec((None, monitor_count, sb), lambda g: (g, 0, 0)),
            pl.BlockSpec((sb, outage_total), lambda g: (g, 0)),
            pl.BlockSpec((monitor_count, outage_total), lambda g: (0, 0)),
            pl.BlockSpec((monitor_count, 1), lambda g: (0, 0)),
        ],
        out_specs=[
            pl.BlockSpec((sb, monitor_count, lanes), lambda g: (g, 0, 0)),
            pl.BlockSpec((sb, outage_total), lambda g: (g, 0)),
        ],
        out_shape=[
            jax.ShapeDtypeStruct((scen_rows, monitor_count, lanes), jnp.float32),
            jax.ShapeDtypeStruct((scen_rows, outage_total), jnp.float32),
        ],
    )(base3, outflow, lodf2, lim2)
    direct = jnp.sum(direct_lanes, axis=2) / (2.0 * outage_total)
    return direct, sens / (2.0 * half)


def exchange_sum(values, axis, count):
    blocks = values.reshape((count, values.shape[0] // count) + values.shape[1:])
    return jnp.sum(lax.all_to_all(blocks, axis, 0, 0, tiled=False), axis=0)


def gather_columns(values, axis, count):
    copies = jnp.broadcast_to(values[None], (count,) + values.shape)
    gathered = lax.all_to_all(copies, axis, 0, 0, tiled=False)
    return gathered.transpose(1, 0, 2).reshape(values.shape[0], count * values.shape[1])


def gather_rows(values, axis):
    count = lax.axis_size(axis)
    copies = jnp.broadcast_to(values[None], (count,) + values.shape)
    gathered = lax.all_to_all(copies, axis, 0, 0, tiled=False)
    return gathered.reshape((count * values.shape[0],) + values.shape[1:])


def line_index():
    index = lax.axis_index(LINE[0])
    for name in LINE[1:]:
        index = index * lax.axis_size(name) + lax.axis_index(name)
    return index


def on_device(
    generation, profiles, scen_profile, ptdf, lodf, limits, monitored, outages, cost_quad
):
    line_count = lax.axis_size(LINE)
    profile_count = profiles.shape[0]
    profile_pick = (
        scen_profile[:, None] == jnp.arange(profile_count, dtype=jnp.int32)[None, :]
    ).astype(jnp.float32)
    loads = jnp.dot(profile_pick, profiles, precision=lax.Precision.HIGHEST)
    injection = (generation.astype(jnp.float32) - loads).astype(jnp.bfloat16)
    scen_rows = injection.shape[0] // lax.axis_size(BUS)
    line_rows = ptdf.shape[0]
    first_line = line_index() * line_rows
    local_monitored = monitored - first_line
    monitor_count = monitored.shape[0]
    outage_total = outages.shape[0]
    monitored_total = monitor_count * line_count

    rel_outages = outages - first_line
    in_block = (rel_outages >= 0) & (rel_outages < line_rows)
    outage_rows = jnp.where(
        in_block[:, None],
        jnp.take(ptdf, jnp.clip(rel_outages, 0, line_rows - 1), axis=0),
        jnp.zeros((), ptdf.dtype),
    )
    staged_order = [lax.axis_size(name) for name in LINE]
    my_outage_rows = (
        outage_rows.reshape(staged_order + [outage_total // line_count, line_rows])
        .transpose(2, 1, 0, 3, 4)
        .reshape(outage_rows.shape)
    )
    for name in LINE[::-1]:
        my_outage_rows = exchange_sum(my_outage_rows, name, lax.axis_size(name))
    monitored_rows = jnp.take(ptdf, local_monitored, axis=0)
    rows = jnp.concatenate([monitored_rows, my_outage_rows], axis=0)

    flow_part = lax.dot_general(
        injection, rows, (((1,), (1,)), ((), ())), preferred_element_type=jnp.float32
    )
    flow_field = exchange_sum(
        exchange_sum(flow_part, "y", lax.axis_size("y")), "zh", lax.axis_size("zh")
    )
    base = flow_field[:, :monitor_count]
    outflow = gather_columns(flow_field[:, monitor_count:], LINE, line_count)

    direct, sens_part = penalty_slopes(base, outflow, lodf, limits)

    matches = (outages[:, None] == monitored[None, :]).astype(jnp.float32)
    flag_part = jnp.sum(matches, axis=1)
    extended = jnp.concatenate(
        [sens_part, flag_part[None, :], jnp.zeros((7, outage_total), jnp.float32)], axis=0
    )
    out_share = outage_total // line_count
    shares = extended.reshape(extended.shape[0], line_count, out_share).transpose(1, 0, 2)
    mine = jnp.sum(lax.all_to_all(shares, LINE, 0, 0, tiled=False), axis=0)
    sens_mine = mine[:scen_rows]
    flag_mine = mine[scen_rows]
    sens_total = gather_columns(sens_mine, LINE, line_count)
    backward = sens_total / outage_total
    outage_sens = sens_total / math.sqrt(monitored_total)

    adjoint_monitored = (
        direct + jnp.dot(backward, matches, precision=lax.Precision.HIGHEST)
    ).astype(jnp.bfloat16)
    adjoint_outage = jnp.where(
        flag_mine[None, :] > 0.5, 0.0, sens_mine / outage_total
    ).astype(jnp.bfloat16)
    piece = jnp.concatenate([adjoint_monitored, adjoint_outage], axis=1)
    all_piece = gather_rows(gather_rows(piece, "zh"), "y")
    grad_rows = all_piece.shape[0] // line_count
    staged_order = [lax.axis_size(name) for name in LINE]
    ordered_piece = (
        all_piece.reshape(staged_order + [grad_rows, all_piece.shape[1]])
        .transpose(2, 1, 0, 3, 4)
        .reshape(all_piece.shape)
    )
    pushed = jnp.dot(ordered_piece, rows, preferred_element_type=jnp.float32)
    for name in LINE[::-1]:
        pushed = exchange_sum(pushed, name, lax.axis_size(name))
    own_generation = lax.dynamic_slice_in_dim(
        generation, line_index() * grad_rows, grad_rows, 0
    ).astype(jnp.float32)
    gradient = (cost_quad[None, :] * own_generation + pushed).astype(jnp.bfloat16)
    return (gradient, outflow, outage_sens)


def solution(mesh):
    fine = Mesh(mesh.devices.reshape(4, 4, 2, 4, 2), BUS + LINE)
    placed = (
        P(None, BUS),
        P(None, BUS),
        P(),
        P(LINE, BUS),
        P(LINE, None),
        P(LINE),
        P(LINE),
        P(),
        P(BUS),
    )
    return jax.shard_map(
        on_device,
        mesh=fine,
        in_specs=placed,
        out_specs=(P(LINE, BUS), P(BUS, None), P(BUS, None)),
        check_vma=False,
    )
```

```python
import math

import jax
import jax.numpy as jnp
from jax import lax
from jax.experimental import pallas as pl
from jax.sharding import Mesh, PartitionSpec as P

sharpness = 4.0
BUS = ("y", "zh")
LINE = ("zl", "x", "core")


def penalty_slopes(base, outflow, lodf, limits):
    scen_rows, monitor_count = base.shape
    outage_total = outflow.shape[1]
    sb = 16
    ch = 16
    lanes = 128
    blocks = scen_rows // sb
    half = sharpness / 2
    base3 = (half * base).reshape(blocks, sb, monitor_count).transpose(0, 2, 1)
    lodf2 = half * lodf
    lim2 = (half * limits).reshape(monitor_count, 1)

    def kernel(base_ref, out_ref, lodf_ref, lim_ref, direct_ref, sens_ref):
        for i in range(sb):
            flow_row = out_ref[i:i + 1, :]

            def body(c, acc):
                r = pl.multiple_of(c * ch, ch)
                weight = lodf_ref[pl.ds(r, ch), :]
                bound = lim_ref[pl.ds(r, ch), :]
                post = base_ref[pl.ds(r, ch), i:i + 1] + weight * flow_row
                slope = jnp.tanh(post - bound) + jnp.tanh(post + bound)
                folded = slope[:, 0:lanes]
                for q in range(1, outage_total // lanes):
                    folded = folded + slope[:, q * lanes:(q + 1) * lanes]
                direct_ref[i, pl.ds(r, ch), :] = folded
                return acc + weight * slope

            acc = lax.fori_loop(0, monitor_count // ch, body,
                                jnp.zeros((ch, outage_total), jnp.float32),
                                unroll=monitor_count // ch)
            sens_ref[i:i + 1, :] = jnp.sum(acc, axis=0, keepdims=True)

    direct_lanes, sens = pl.pallas_call(
        kernel,
        grid=(blocks,),
        in_specs=[
            pl.BlockSpec((None, monitor_count, sb), lambda g: (g, 0, 0)),
            pl.BlockSpec((sb, outage_total), lambda g: (g, 0)),
            pl.BlockSpec((monitor_count, outage_total), lambda g: (0, 0)),
            pl.BlockSpec((monitor_count, 1), lambda g: (0, 0)),
        ],
        out_specs=[
            pl.BlockSpec((sb, monitor_count, lanes), lambda g: (g, 0, 0)),
            pl.BlockSpec((sb, outage_total), lambda g: (g, 0)),
        ],
        out_shape=[
            jax.ShapeDtypeStruct((scen_rows, monitor_count, lanes), jnp.float32),
            jax.ShapeDtypeStruct((scen_rows, outage_total), jnp.float32),
        ],
    )(base3, outflow, lodf2, lim2)
    direct = jnp.sum(direct_lanes, axis=2) / (2.0 * outage_total)
    return direct, sens / (2.0 * half)


def exchange_sum(values, axis, count):
    blocks = values.reshape((count, values.shape[0] // count) + values.shape[1:])
    return jnp.sum(lax.all_to_all(blocks, axis, 0, 0, tiled=False), axis=0)


def gather_columns(values, axis, count):
    copies = jnp.broadcast_to(values[None], (count,) + values.shape)
    gathered = lax.all_to_all(copies, axis, 0, 0, tiled=False)
    return gathered.transpose(1, 0, 2).reshape(values.shape[0], count * values.shape[1])


def gather_rows(values, axis):
    count = lax.axis_size(axis)
    copies = jnp.broadcast_to(values[None], (count,) + values.shape)
    gathered = lax.all_to_all(copies, axis, 0, 0, tiled=False)
    return gathered.reshape((count * values.shape[0],) + values.shape[1:])


def line_index():
    index = lax.axis_index(LINE[0])
    for name in LINE[1:]:
        index = index * lax.axis_size(name) + lax.axis_index(name)
    return index


def on_device(
    generation, profiles, scen_profile, ptdf, lodf, limits, monitored, outages, cost_quad
):
    line_count = lax.axis_size(LINE)
    profile_count = profiles.shape[0]
    profile_pick = (
        scen_profile[:, None] == jnp.arange(profile_count, dtype=jnp.int32)[None, :]
    ).astype(jnp.float32)
    loads = jnp.dot(profile_pick, profiles, precision=lax.Precision.HIGHEST)
    injection = (generation.astype(jnp.float32) - loads).astype(jnp.bfloat16)
    scen_rows = injection.shape[0] // lax.axis_size(BUS)
    line_rows = ptdf.shape[0]
    first_line = line_index() * line_rows
    local_monitored = monitored - first_line
    monitor_count = monitored.shape[0]
    outage_total = outages.shape[0]
    monitored_total = monitor_count * line_count

    rel_outages = outages - first_line
    in_block = (rel_outages >= 0) & (rel_outages < line_rows)
    outage_rows = jnp.where(
        in_block[:, None],
        jnp.take(ptdf, jnp.clip(rel_outages, 0, line_rows - 1), axis=0),
        jnp.zeros((), ptdf.dtype),
    )
    my_outage_rows = exchange_sum(outage_rows, LINE, line_count)
    monitored_rows = jnp.take(ptdf, local_monitored, axis=0)
    rows = jnp.concatenate([monitored_rows, my_outage_rows], axis=0)

    flow_part = lax.dot_general(
        injection, rows, (((1,), (1,)), ((), ())), preferred_element_type=jnp.float32
    )
    flow_field = exchange_sum(
        exchange_sum(flow_part, "y", lax.axis_size("y")), "zh", lax.axis_size("zh")
    )
    base = flow_field[:, :monitor_count]
    outflow = gather_columns(flow_field[:, monitor_count:], LINE, line_count)

    direct, sens_part = penalty_slopes(base, outflow, lodf, limits)

    matches = (outages[:, None] == monitored[None, :]).astype(jnp.float32)
    flag_part = jnp.sum(matches, axis=1)
    extended = jnp.concatenate(
        [sens_part, flag_part[None, :], jnp.zeros((7, outage_total), jnp.float32)], axis=0
    )
    out_share = outage_total // line_count
    shares = extended.reshape(extended.shape[0], line_count, out_share).transpose(1, 0, 2)
    mine = jnp.sum(lax.all_to_all(shares, LINE, 0, 0, tiled=False), axis=0)
    sens_mine = mine[:scen_rows]
    flag_mine = mine[scen_rows]
    sens_total = gather_columns(sens_mine, LINE, line_count)
    backward = sens_total / outage_total
    outage_sens = sens_total / math.sqrt(monitored_total)

    adjoint_monitored = (
        direct + jnp.dot(backward, matches, precision=lax.Precision.HIGHEST)
    ).astype(jnp.bfloat16)
    adjoint_outage = jnp.where(
        flag_mine[None, :] > 0.5, 0.0, sens_mine / outage_total
    ).astype(jnp.bfloat16)
    piece = jnp.concatenate([adjoint_monitored, adjoint_outage], axis=1)
    all_piece = gather_rows(gather_rows(piece, "zh"), "y")
    grad_rows = all_piece.shape[0] // line_count
    staged_order = [lax.axis_size(name) for name in LINE]
    ordered_piece = (
        all_piece.reshape(staged_order + [grad_rows, all_piece.shape[1]])
        .transpose(2, 1, 0, 3, 4)
        .reshape(all_piece.shape)
    )
    pushed = jnp.dot(ordered_piece, rows, preferred_element_type=jnp.float32)
    for name in LINE[::-1]:
        pushed = exchange_sum(pushed, name, lax.axis_size(name))
    own_generation = lax.dynamic_slice_in_dim(
        generation, line_index() * grad_rows, grad_rows, 0
    ).astype(jnp.float32)
    gradient = (cost_quad[None, :] * own_generation + pushed).astype(jnp.bfloat16)
    return (gradient, outflow, outage_sens)


def solution(mesh):
    fine = Mesh(mesh.devices.reshape(4, 4, 2, 4, 2), BUS + LINE)
    placed = (
        P(None, BUS),
        P(None, BUS),
        P(),
        P(LINE, BUS),
        P(LINE, None),
        P(LINE),
        P(LINE),
        P(),
        P(BUS),
    )
    return jax.shard_map(
        on_device,
        mesh=fine,
        in_specs=placed,
        out_specs=(P(LINE, BUS), P(BUS, None), P(BUS, None)),
        check_vma=False,
    )
```
